256 devices in a mesh: expert: 64 (over z, y, x_hi), tensor: 4 (over x_lo, core).
Axes of the slice: x: 4 (x_hi: 2, x_lo: 2; x = x_hi * 2 + x_lo), y: 4, z: 8, core: 2. Of those that a mesh axis runs over, the one named last changes fastest.
Arguments:
- attn_partial: bfloat16 [4, 8192, 4096], P('tensor', 'expert'), may hold values from -4 to 4
- residual: bfloat16 [8192, 4096], P('expert', 'tensor'), may hold values from -40 to 40
- norm_gain: float32 [4096], P('tensor'), may hold values from 0.1 to 1.9
- expert_ids: int32 [8192, 4], P('expert'), may hold values from 0 to 63, all different within a row; in each aligned block of 128 rows (0 to 127, 128 to 255, ...) at most 10 rows name the same one
- route_weight: float32 [8192, 4], P('expert'), may hold values from 0.1 to 1
- w_in: bfloat16 [64, 4096, 2048], P('expert', 'tensor'), may hold values from -0.09375 to 0.09375
- w_down: bfloat16 [64, 1024, 4096], P('expert', None, 'tensor'), may hold values from -0.1875 to 0.1875
Outputs:
- layer_out: bfloat16 [8192, 4096], P('expert', 'tensor')
The draws below stay inside these ranges and needn't reach their ends.
Inputs may be any that keep to these rules, and one draw needn't show every extreme that they name: `expert_ids`: in each aligned block of 128 rows (the tokens of one index of expert) no expert is named by more than 10 rows, a bound that some block reaches. A row names 4 different experts.
All inputs are finite; a program needn't handle non-finite values.
Results may differ from the reference program's by a relative error of at most 0.01.
Values may be sent and summed in bfloat16 or wider, within the bound.
No kernel may reach another device: no remote copies, remote signals or barrier semaphores. Data moves between devices by JAX's collectives and lax.ppermute only.
A program may use at most 64 MiB of HBM per device.

```python
import math
import jax
import jax.numpy as jnp
import numpy as np
from jax import lax

D = 4096
FF = 1024
TOPK = 4
TOKG = 128
EXPERTS = 64
CAP = 10
TOKENS = 8192
N_TENSOR = 4


def draw_residual(key, part):
    first, second = jax.random.split(key, 2)
    column = jnp.arange(D, dtype=jnp.float32)
    rising = 1.0 + 2.0 * column / D
    spread = jnp.exp(jax.random.uniform(second, (D,), jnp.float32) * math.log(10.0))
    colscale = rising * spread / 6.0
    values = jax.random.normal(first, (TOKENS, D), jnp.float32) * colscale
    return jnp.clip(values, -40.0, 40.0).astype(jnp.bfloat16)


def spiked(values, own_key, source, target, shards_of, factor):
    owner, partner = [(jnp.arange(values.shape[axis_at]) // (values.shape[axis_at] // shards_of)).reshape([-1 if axis == axis_at else 1 for axis in range(values.ndim)]) for axis_at in (source, target)]
    chosen = jax.random.permutation(own_key, shards_of)[partner]
    strong = (owner == chosen) | (owner == (partner + shards_of // 2) % shards_of)
    return jnp.where(strong, factor * values, values)


def block_scale(stream_key, extent, cuts, low, largest):
    loudness = 1.0
    for axis_at, blocks in cuts:
        steps = jax.random.uniform(jax.random.fold_in(jax.random.fold_in(stream_key, 6), axis_at), (blocks,), jnp.float32, low / len(cuts), largest / len(cuts))
        loudness = loudness * jnp.repeat(jnp.exp(steps), extent[axis_at] // blocks).reshape((-1,) + (1,) * (len(extent) - 1 - axis_at))
    return loudness


def deal_out(rng, own, number, rows, number_of, top, reach, skew):
    ranking = jax.random.permutation(rng, number_of)
    heavy_load, usual = portions_of(number_of, rows * top, reach, skew, True), portions_of(number_of, rows * top, reach, skew, False)
    places = jnp.arange(number_of)

    def named(sizes, turn):
        used = int((sizes > 0).sum())
        fixed = max(1, used // 4)
        moved = fixed + (places - fixed + turn * (used - fixed)) % max(1, number_of - fixed)
        return jnp.zeros((number_of,), jnp.int32).at[ranking[jnp.where(places < fixed, places, moved)]].set(jnp.asarray(sizes, jnp.int32))

    sizes = jnp.where(number % 4 == 0, named(heavy_load, number // 4), named(usual, number - number // 4 - 1))
    mixed = jax.random.permutation(jax.random.fold_in(own, 3), number_of)
    giver, sink = mixed[0:number_of // 2 * 2:2], mixed[1:number_of // 2 * 2:2]
    room = jnp.minimum(sizes[giver] - 1, reach - sizes[sink]) // 2
    room = jnp.where((giver == ranking[0]) | (sink == ranking[0]) | (sizes[sink] == 0), 0, jnp.maximum(room, 0))
    moved = jax.random.randint(jax.random.fold_in(own, 4), (number_of // 2,), 0, 1 << 20) % (room + 1)
    sizes = sizes.at[giver].add(-moved).at[sink].add(moved)
    items = jnp.searchsorted(jnp.cumsum(sizes), jnp.arange(rows * top), side="right").astype(jnp.int32)
    listing = items.reshape(top, rows).T
    listing = listing[jax.random.permutation(jax.random.fold_in(own, 1), rows)]
    turn = jax.random.randint(jax.random.fold_in(own, 2), (rows, 1), 0, top)
    return jnp.take_along_axis(listing, (jnp.arange(top)[None, :] + turn) % top, axis=1)


def portions_of(number_of, total, reach, slope, full):
    weights = [(1 << 20) // math.isqrt(standing ** slope) + 1 for standing in range(1, number_of + 1)]
    largest = reach if full else min(reach, max(-(-total // number_of), total * weights[0] // sum(weights)))
    least = 1 if total - largest >= number_of - 1 else 0
    given, rest = [largest] + [least] * (number_of - 1), total - largest - least * (number_of - 1)
    while rest > 0:
        candidates = [i for i in range(1, number_of) if given[i] < largest] or [i for i in range(1, number_of) if given[i] < reach]
        pool, left = sum([weights[i] for i in candidates]), rest
        for i in candidates:
            addition = min(reach - given[i], max(1, left * weights[i] // pool), rest)
            given[i] = given[i] + addition
            rest = rest - addition
    return np.array(given)


def bell_draw(stream_key, shape, scale, bound, pieces=(), kind=jnp.bfloat16):
    drawn = jax.random.normal(stream_key, shape, jnp.float32) * scale
    if len(pieces) > 0:
        drawn = block_scale(stream_key, shape, pieces, -0.22, 0.18) * drawn
    return jnp.clip(drawn, min=-bound, max=bound).astype(kind)


def bell_draw_with(own_key, dims, deviation, most, cuts, heavy, kind=jnp.bfloat16):
    result = deviation * jax.random.normal(own_key, dims, jnp.float32)
    if cuts:
        result = result * block_scale(own_key, dims, cuts, -0.22, 0.18)
    return jnp.clip(spiked(result, jax.random.fold_in(own_key, 3), *heavy), -most, most).astype(kind)


def setup_inputs(seed: int = 0) -> dict:
    keys = jax.random.split(jax.random.key(seed), 8)
    attn_partial = bell_draw_with(keys[0], (N_TENSOR, TOKENS, D), 0.2, 4.0, ((0, 4), (1, 64)), (0, 2, 4, 2.0))
    residual = draw_residual(jax.random.fold_in(keys[7], 71), 0)
    norm_gain = jnp.clip(1.0 + 0.18 * jax.random.normal(keys[2], (D,), jnp.float32), 0.1, 1.9)
    expert_ids_keys = jax.random.split(jax.random.fold_in(keys[3], 1), TOKENS // TOKG)
    expert_ids_turns = jax.random.permutation(jax.random.fold_in(keys[3], 3), TOKENS // TOKG)
    expert_ids = jax.vmap(lambda own, number: deal_out(jax.random.fold_in(keys[3], 2), own, number, TOKG, EXPERTS, TOPK, CAP, 2))(expert_ids_keys, expert_ids_turns).reshape((TOKENS, TOPK))
    route_weight = jnp.clip(0.1 + 0.9 * jax.random.uniform(keys[4], (TOKENS, TOPK), jnp.float32) ** block_scale(keys[4], (TOKENS, TOPK), ((0, 64),), -0.2, 0.2), 0.1, 1.0)
    w_in = bell_draw(keys[5], (EXPERTS, D, 2 * FF), D ** -0.5, 0.09375, ((0, 64), (1, 4)))
    w_down = bell_draw(keys[6], (EXPERTS, FF, D), FF ** -0.5, 0.1875, ((0, 64), (2, 4)))
    return dict(attn_partial=attn_partial, residual=residual, norm_gain=norm_gain, expert_ids=expert_ids, route_weight=route_weight, w_in=w_in, w_down=w_down)


def reference(attn_partial, residual, norm_gain, expert_ids, route_weight, w_in, w_down):
    attention = lax.optimization_barrier(jnp.sum(attn_partial.astype(jnp.float32), axis=0))
    stream = residual.astype(jnp.float32) + attention
    inverse = lax.rsqrt(lax.optimization_barrier(jnp.mean(stream * stream, axis=1, keepdims=True)) + 1e-06)
    normed = stream * inverse * norm_gain[None, :]
    rows = normed.astype(jnp.bfloat16)
    group_count = TOKENS // TOKG
    flat_ids = expert_ids.reshape(group_count, TOKG * TOPK).astype(jnp.int32)
    one_hot = (flat_ids[:, :, None] == jnp.arange(EXPERTS, dtype=jnp.int32)[None, None, :]).astype(jnp.int32)
    earlier = jnp.cumsum(one_hot, axis=1) - one_hot
    slot_index = lax.optimization_barrier(jnp.sum(earlier * one_hot, axis=2)).astype(jnp.int32)
    source = jnp.arange(group_count, dtype=jnp.int32)[:, None]
    token_of = (source * TOKG + jnp.arange(TOKG * TOPK, dtype=jnp.int32)[None, :] // TOPK).astype(jnp.int32)
    columns = (source * CAP + slot_index).astype(jnp.int32)
    row_table = jnp.zeros((EXPERTS, group_count * CAP), jnp.int32).at[flat_ids, columns].set(token_of)

    def run_expert(expert):
        row_data = rows[row_table[expert]].astype(jnp.float32).reshape(-1, N_TENSOR, D // N_TENSOR)
        weight_in = w_in[expert].astype(jnp.float32).reshape(N_TENSOR, D // N_TENSOR, 2 * FF)
        partial_value = jnp.einsum('rif,ifo->rio', row_data, weight_in, precision=lax.Precision.HIGHEST)
        rounded = lax.optimization_barrier(partial_value.astype(jnp.bfloat16))
        summed = lax.optimization_barrier(jnp.sum(rounded.astype(jnp.float32), axis=1))
        hidden = (jax.nn.silu(summed[:, :FF]) * summed[:, FF:]).astype(jnp.bfloat16)
        return jnp.dot(hidden, w_down[expert], preferred_element_type=jnp.float32).astype(jnp.bfloat16)
    results = lax.map(run_expert, jnp.arange(EXPERTS, dtype=jnp.int32))
    picked = results[flat_ids, columns].astype(jnp.float32).reshape(TOKENS, TOPK, D)
    routed = lax.optimization_barrier(jnp.sum(route_weight[:, :, None] * picked, axis=1))
    return (stream + routed).astype(jnp.bfloat16)
```

```python
import jax
import jax.numpy as jnp
from jax import lax
from jax.sharding import PartitionSpec as P


def body(attn_partial, residual, norm_gain, expert_ids, route_weight, w_in, w_down):
    token_count = expert_ids.shape[0]
    topk_count = expert_ids.shape[1]
    feature_local = residual.shape[1]
    feature_count = feature_local * lax.axis_size("tensor")
    hidden_width = w_down.shape[1]
    expert_count = lax.axis_size("expert")
    capacity = 5 * token_count * topk_count // (4 * expert_count)
    attention = lax.psum_scatter(
        attn_partial[0].astype(jnp.float32).astype(jnp.bfloat16),
        "tensor",
        scatter_dimension=1,
        tiled=True,
    ).astype(jnp.float32)
    stream = residual.astype(jnp.float32) + attention
    squares = lax.psum(jnp.sum(stream * stream, axis=1), "tensor")
    inverse = lax.rsqrt(squares / feature_count + 1e-06)[:, None]
    normed = stream * inverse * norm_gain[None, :]
    rows = normed.astype(jnp.bfloat16)
    flat_ids = expert_ids.reshape(-1)
    one_hot = (flat_ids[:, None] == jnp.arange(expert_count, dtype=jnp.int32)[None, :]).astype(
        jnp.int32
    )
    earlier = jnp.cumsum(one_hot, axis=0) - one_hot
    slot_index = jnp.sum(earlier * one_hot, axis=1)
    positions = (flat_ids * capacity + slot_index).reshape(token_count, topk_count)
    places = jnp.arange(expert_count * capacity, dtype=jnp.int32)
    matches = positions[None, :, :] == places[:, None, None]
    dispatch = jnp.any(matches, axis=2)
    sent_rows = jnp.dot(dispatch.astype(jnp.bfloat16), rows, preferred_element_type=jnp.float32)
    sent_rows = sent_rows.astype(jnp.bfloat16).reshape(expert_count, capacity, feature_local)
    weights_table = jnp.sum(jnp.where(matches, route_weight[None, :, :], 0.0), axis=2).T
    in_rows = lax.all_to_all(sent_rows, "expert", split_axis=0, concat_axis=0, tiled=True)
    source_count = in_rows.shape[0]
    item_count = in_rows.shape[1]
    row_total = source_count * item_count
    flat_rows = in_rows.reshape(row_total, feature_local)
    partial_value = jnp.dot(flat_rows, w_in[0], preferred_element_type=jnp.float32)
    total = lax.psum_scatter(
        partial_value.astype(jnp.bfloat16), "tensor", scatter_dimension=0, tiled=True
    ).astype(jnp.float32)
    hidden = (jax.nn.silu(total[:, :hidden_width]) * total[:, hidden_width:]).astype(jnp.bfloat16)
    hidden = lax.all_gather(hidden, "tensor", axis=0, tiled=True)
    produced = jnp.dot(hidden, w_down[0], preferred_element_type=jnp.float32).astype(jnp.bfloat16)
    results = produced.reshape(source_count, item_count, feature_local)
    returned = lax.all_to_all(results, "expert", split_axis=0, concat_axis=0, tiled=True)
    routed = jnp.dot(
        weights_table,
        returned.reshape(expert_count * capacity, feature_local).astype(jnp.float32),
        precision=lax.Precision.HIGHEST,
    )
    return (stream + routed).astype(jnp.bfloat16)


def solution(mesh):
    in_specs = (
        P("tensor", "expert", None),
        P("expert", "tensor"),
        P("tensor"),
        P("expert", None),
        P("expert", None),
        P("expert", "tensor", None),
        P("expert", None, "tensor"),
    )
    out_specs = P("expert", "tensor")
    return jax.shard_map(body, mesh=mesh, in_specs=in_specs, out_specs=out_specs, check_vma=False)
```

```python
import jax
import jax.numpy as jnp
from jax import lax
from jax.sharding import PartitionSpec as P


def _exchange(value, flip):
    size = lax.axis_size("tensor")
    return lax.ppermute(value, "tensor", [(j, j ^ flip) for j in range(size)])


def _pick(value, axis, index):
    return lax.dynamic_index_in_dim(value, index, axis=axis, keepdims=False)


def _reduce_scatter(value, axis):
    t = lax.axis_index("tensor")
    core = t % 2
    high = t // 2
    shape = value.shape
    split = value.reshape(shape[:axis] + (2, 2, shape[axis] // 4) + shape[axis + 1:])
    sent = _pick(split, axis + 1, 1 - core).astype(jnp.bfloat16)
    kept = _pick(split, axis + 1, core).astype(jnp.float32)
    half = kept + _exchange(sent, 1).astype(jnp.float32)
    sent = _pick(half, axis, 1 - high).astype(jnp.bfloat16)
    kept = _pick(half, axis, high)
    return kept + _exchange(sent, 2).astype(jnp.float32)


def _all_gather(value, axis):
    t = lax.axis_index("tensor")
    core = t % 2
    high = t // 2
    other = _exchange(value, 2)
    pair = jnp.where(high == 0, jnp.stack([value, other], axis), jnp.stack([other, value], axis))
    other = _exchange(pair, 1)
    quad = jnp.where(core == 0, jnp.stack([pair, other], axis + 1), jnp.stack([other, pair], axis + 1))
    shape = quad.shape
    return quad.reshape(shape[:axis] + (shape[axis] * shape[axis + 1] * shape[axis + 2],) + shape[axis + 3:])


def _psum(value):
    value = value + _exchange(value, 1)
    return value + _exchange(value, 2)


def body(attn_partial, residual, norm_gain, expert_ids, route_weight, w_in, w_down):
    token_count = expert_ids.shape[0]
    topk_count = expert_ids.shape[1]
    feature_local = residual.shape[1]
    feature_count = feature_local * lax.axis_size("tensor")
    hidden_width = w_down.shape[1]
    expert_count = lax.axis_size("expert")
    capacity = 5 * token_count * topk_count // (4 * expert_count)
    attention = _reduce_scatter(attn_partial[0], 1)
    stream = residual.astype(jnp.float32) + attention
    squares = _psum(jnp.sum(stream * stream, axis=1))
    inverse = lax.rsqrt(squares / feature_count + 1e-06)[:, None]
    normed = stream * inverse * norm_gain[None, :]
    rows = normed.astype(jnp.bfloat16)
    flat_ids = expert_ids.reshape(-1)
    one_hot = (flat_ids[:, None] == jnp.arange(expert_count, dtype=jnp.int32)[None, :]).astype(
        jnp.int32
    )
    earlier = jnp.cumsum(one_hot, axis=0) - one_hot
    slot_index = jnp.sum(earlier * one_hot, axis=1)
    positions = (flat_ids * capacity + slot_index).reshape(token_count, topk_count)
    places = jnp.arange(expert_count * capacity, dtype=jnp.int32)
    matches = positions[None, :, :] == places[:, None, None]
    dispatch = jnp.any(matches, axis=2)
    sent_rows = jnp.dot(dispatch.astype(jnp.bfloat16), rows, preferred_element_type=jnp.float32)
    sent_rows = sent_rows.astype(jnp.bfloat16).reshape(expert_count, capacity, feature_local)
    weights_table = jnp.sum(jnp.where(matches, route_weight[None, :, :], 0.0), axis=2).T
    in_rows = lax.all_to_all(sent_rows, "expert", split_axis=0, concat_axis=0, tiled=True)
    source_count = in_rows.shape[0]
    item_count = in_rows.shape[1]
    row_total = source_count * item_count
    flat_rows = in_rows.reshape(row_total, feature_local)
    partial_value = jnp.dot(flat_rows, w_in[0], preferred_element_type=jnp.float32)
    total = _reduce_scatter(partial_value.astype(jnp.bfloat16), 0)
    hidden = (jax.nn.silu(total[:, :hidden_width]) * total[:, hidden_width:]).astype(jnp.bfloat16)
    hidden = _all_gather(hidden, 0)
    produced = jnp.dot(hidden, w_down[0], preferred_element_type=jnp.float32).astype(jnp.bfloat16)
    results = produced.reshape(source_count, item_count, feature_local)
    returned = lax.all_to_all(results, "expert", split_axis=0, concat_axis=0, tiled=True)
    routed = jnp.dot(
        weights_table,
        returned.reshape(expert_count * capacity, feature_local).astype(jnp.float32),
        precision=lax.Precision.HIGHEST,
    )
    return (stream + routed).astype(jnp.bfloat16)


def solution(mesh):
    in_specs = (
        P("tensor", "expert", None),
        P("expert", "tensor"),
        P("tensor"),
        P("expert", None),
        P("expert", None),
        P("expert", "tensor", None),
        P("expert", None, "tensor"),
    )
    out_specs = P("expert", "tensor")
    return jax.shard_map(body, mesh=mesh, in_specs=in_specs, out_specs=out_specs, check_vma=False)
```

```python
import jax
import jax.numpy as jnp
from jax import lax
from jax.sharding import PartitionSpec as P


def _exchange(value, flip):
    size = lax.axis_size("tensor")
    return lax.ppermute(value, "tensor", [(j, j ^ flip) for j in range(size)])


def _pick(value, axis, index):
    return lax.dynamic_index_in_dim(value, index, axis=axis, keepdims=False)


def _reduce_scatter(value, axis):
    t = lax.axis_index("tensor")
    core = t % 2
    high = t // 2
    shape = value.shape
    split = value.reshape(shape[:axis] + (2, 2, shape[axis] // 4) + shape[axis + 1:])
    sent = _pick(split, axis + 1, 1 - core).astype(jnp.bfloat16)
    kept = _pick(split, axis + 1, core).astype(jnp.float32)
    half = kept + _exchange(sent, 1).astype(jnp.float32)
    sent = _pick(half, axis, 1 - high).astype(jnp.bfloat16)
    kept = _pick(half, axis, high)
    return kept + _exchange(sent, 2).astype(jnp.float32)


def _all_gather(value, axis):
    t = lax.axis_index("tensor")
    core = t % 2
    high = t // 2
    other = _exchange(value, 2)
    pair = jnp.where(high == 0, jnp.stack([value, other], axis), jnp.stack([other, value], axis))
    other = _exchange(pair, 1)
    quad = jnp.where(core == 0, jnp.stack([pair, other], axis + 1), jnp.stack([other, pair], axis + 1))
    shape = quad.shape
    return quad.reshape(shape[:axis] + (shape[axis] * shape[axis + 1] * shape[axis + 2],) + shape[axis + 3:])


def _exchange_rows(value):
    experts, slots, features = value.shape
    lanes = features
    while lanes > 128 and (slots * features // lanes) % 8 != 0:
        lanes //= 2
    packed = value.reshape(experts, slots * features // lanes, lanes)
    moved = lax.all_to_all(packed, "expert", split_axis=0, concat_axis=0, tiled=True)
    return moved.reshape(experts, slots, features)


def _psum(value):
    value = value + _exchange(value, 1)
    return value + _exchange(value, 2)


def body(attn_partial, residual, norm_gain, expert_ids, route_weight, w_in, w_down):
    token_count = expert_ids.shape[0]
    topk_count = expert_ids.shape[1]
    feature_local = residual.shape[1]
    feature_count = feature_local * lax.axis_size("tensor")
    hidden_width = w_down.shape[1]
    expert_count = lax.axis_size("expert")
    capacity = 5 * token_count * topk_count // (4 * expert_count)
    attention = _reduce_scatter(attn_partial[0], 1)
    stream = residual.astype(jnp.float32) + attention
    squares = _psum(jnp.sum(stream * stream, axis=1))
    inverse = lax.rsqrt(squares / feature_count + 1e-06)[:, None]
    normed = stream * inverse * norm_gain[None, :]
    rows = normed.astype(jnp.bfloat16)
    flat_ids = expert_ids.reshape(-1)
    one_hot = (flat_ids[:, None] == jnp.arange(expert_count, dtype=jnp.int32)[None, :]).astype(
        jnp.int32
    )
    earlier = jnp.cumsum(one_hot, axis=0) - one_hot
    slot_index = jnp.sum(earlier * one_hot, axis=1)
    positions = (flat_ids * capacity + slot_index).reshape(token_count, topk_count)
    places = jnp.arange(expert_count * capacity, dtype=jnp.int32)
    matches = positions[None, :, :] == places[:, None, None]
    dispatch = jnp.any(matches, axis=2)
    sent_rows = jnp.dot(dispatch.astype(jnp.bfloat16), rows, preferred_element_type=jnp.float32)
    sent_rows = sent_rows.astype(jnp.bfloat16).reshape(expert_count, capacity, feature_local)
    weights_table = jnp.sum(jnp.where(matches, route_weight[None, :, :], 0.0), axis=2).T
    in_rows = _exchange_rows(sent_rows)
    source_count = in_rows.shape[0]
    item_count = in_rows.shape[1]
    row_total = source_count * item_count
    flat_rows = in_rows.reshape(row_total, feature_local)
    partial_value = jnp.dot(flat_rows, w_in[0], preferred_element_type=jnp.float32)
    total = _reduce_scatter(partial_value.astype(jnp.bfloat16), 0)
    hidden = (jax.nn.silu(total[:, :hidden_width]) * total[:, hidden_width:]).astype(jnp.bfloat16)
    hidden = _all_gather(hidden, 0)
    produced = jnp.dot(hidden, w_down[0], preferred_element_type=jnp.float32).astype(jnp.bfloat16)
    results = produced.reshape(source_count, item_count, feature_local)
    returned = _exchange_rows(results)
    routed = jnp.dot(
        weights_table,
        returned.reshape(expert_count * capacity, feature_local).astype(jnp.float32),
        precision=lax.Precision.HIGHEST,
    )
    return (stream + routed).astype(jnp.bfloat16)


def solution(mesh):
    in_specs = (
        P("tensor", "expert", None),
        P("expert", "tensor"),
        P("tensor"),
        P("expert", None),
        P("expert", None),
        P("expert", "tensor", None),
        P("expert", None, "tensor"),
    )
    out_specs = P("expert", "tensor")
    return jax.shard_map(body, mesh=mesh, in_specs=in_specs, out_specs=out_specs, check_vma=False)
```

```python
import jax
import jax.numpy as jnp
from jax import lax
from jax.sharding import PartitionSpec as P


def _exchange(value, flip):
    size = lax.axis_size("tensor")
    return lax.ppermute(value, "tensor", [(j, j ^ flip) for j in range(size)])


def _pick(value, axis, index):
    return lax.dynamic_index_in_dim(value, index, axis=axis, keepdims=False)


def _slab(value, start, size, axis):
    return lax.dynamic_slice_in_dim(value, start, size, axis=axis)


def _reduce_scatter(value, axis):
    t = lax.axis_index("tensor")
    core = t % 2
    high = t // 2
    n = value.shape[axis] // 4
    sent = jnp.concatenate(
        [_slab(value, (1 - core) * n, n, axis), _slab(value, (3 - core) * n, n, axis)], axis
    ).astype(jnp.bfloat16)
    kept = jnp.concatenate([_slab(value, core * n, n, axis), _slab(value, (2 + core) * n, n, axis)], axis)
    half = kept.astype(jnp.float32) + _exchange(sent, 1).astype(jnp.float32)
    sent = _slab(half, (1 - high) * n, n, axis).astype(jnp.bfloat16)
    kept = _slab(half, high * n, n, axis)
    return kept + _exchange(sent, 2).astype(jnp.float32)


def _all_gather(value, axis):
    t = lax.axis_index("tensor")
    core = t % 2
    high = t // 2
    n = value.shape[axis]
    shape = list(value.shape)
    shape[axis] = 2 * n
    pair = jnp.zeros(shape, value.dtype)
    pair = lax.dynamic_update_slice_in_dim(pair, value, high * n, axis)
    pair = lax.dynamic_update_slice_in_dim(pair, _exchange(value, 2), (1 - high) * n, axis)
    other = _exchange(pair, 1)
    shape[axis] = 4 * n
    full = jnp.zeros(shape, value.dtype)
    for part, side in ((pair, core), (other, 1 - core)):
        for a in range(2):
            full = lax.dynamic_update_slice_in_dim(full, _slab(part, a * n, n, axis), (2 * a + side) * n, axis)
    return full


def _exchange_rows(value):
    experts, slots, features = value.shape
    lanes = features
    while lanes > 128 and (slots * features // lanes) % 8 != 0:
        lanes //= 2
    packed = value.reshape(experts, slots * features // lanes, lanes)
    moved = lax.all_to_all(packed, "expert", split_axis=0, concat_axis=0, tiled=True)
    return moved.reshape(experts, slots, features)


def _psum(value):
    value = value + _exchange(value, 1)
    return value + _exchange(value, 2)


def body(attn_partial, residual, norm_gain, expert_ids, route_weight, w_in, w_down):
    token_count = expert_ids.shape[0]
    topk_count = expert_ids.shape[1]
    feature_local = residual.shape[1]
    feature_count = feature_local * lax.axis_size("tensor")
    hidden_width = w_down.shape[1]
    expert_count = lax.axis_size("expert")
    capacity = 5 * token_count * topk_count // (4 * expert_count)
    attention = _reduce_scatter(attn_partial[0], 1)
    stream = residual.astype(jnp.float32) + attention
    squares = _psum(jnp.sum(stream * stream, axis=1))
    inverse = lax.rsqrt(squares / feature_count + 1e-06)[:, None]
    normed = stream * inverse * norm_gain[None, :]
    rows = normed.astype(jnp.bfloat16)
    flat_ids = expert_ids.reshape(-1)
    one_hot = (flat_ids[:, None] == jnp.arange(expert_count, dtype=jnp.int32)[None, :]).astype(
        jnp.int32
    )
    earlier = jnp.cumsum(one_hot, axis=0) - one_hot
    slot_index = jnp.sum(earlier * one_hot, axis=1)
    positions = (flat_ids * capacity + slot_index).reshape(token_count, topk_count)
    places = jnp.arange(expert_count * capacity, dtype=jnp.int32)
    matches = positions[None, :, :] == places[:, None, None]
    dispatch = jnp.any(matches, axis=2)
    sent_rows = jnp.dot(dispatch.astype(jnp.bfloat16), rows, preferred_element_type=jnp.float32)
    sent_rows = sent_rows.astype(jnp.bfloat16).reshape(expert_count, capacity, feature_local)
    weights_table = jnp.sum(jnp.where(matches, route_weight[None, :, :], 0.0), axis=2).T
    in_rows = _exchange_rows(sent_rows)
    source_count = in_rows.shape[0]
    item_count = in_rows.shape[1]
    row_total = source_count * item_count
    flat_rows = in_rows.reshape(row_total, feature_local)
    partial_value = jnp.dot(flat_rows, w_in[0], preferred_element_type=jnp.float32)
    total = _reduce_scatter(partial_value.astype(jnp.bfloat16), 0)
    hidden = (jax.nn.silu(total[:, :hidden_width]) * total[:, hidden_width:]).astype(jnp.bfloat16)
    hidden = _all_gather(hidden, 0)
    produced = jnp.dot(hidden, w_down[0], preferred_element_type=jnp.float32).astype(jnp.bfloat16)
    results = produced.reshape(source_count, item_count, feature_local)
    returned = _exchange_rows(results)
    routed = jnp.dot(
        weights_table,
        returned.reshape(expert_count * capacity, feature_local).astype(jnp.float32),
        precision=lax.Precision.HIGHEST,
    )
    return (stream + routed).astype(jnp.bfloat16)


def solution(mesh):
    in_specs = (
        P("tensor", "expert", None),
        P("expert", "tensor"),
        P("tensor"),
        P("expert", None),
        P("expert", None),
        P("expert", "tensor", None),
        P("expert", None, "tensor"),
    )
    out_specs = P("expert", "tensor")
    return jax.shard_map(body, mesh=mesh, in_specs=in_specs, out_specs=out_specs, check_vma=False)
```

```python
import jax
import jax.numpy as jnp
from jax import lax
from jax.sharding import PartitionSpec as P


def _exchange(value, flip):
    size = lax.axis_size("tensor")
    return lax.ppermute(value, "tensor", [(j, j ^ flip) for j in range(size)])


def _pick(value, axis, index):
    return lax.dynamic_index_in_dim(value, index, axis=axis, keepdims=False)


def _slab(value, start, size, axis):
    return lax.dynamic_slice_in_dim(value, start, size, axis=axis)


def _reduce_scatter(value, axis):
    t = lax.axis_index("tensor")
    core = t % 2
    high = t // 2
    n = value.shape[axis] // 4
    sent = jnp.concatenate(
        [_slab(value, (1 - core) * n, n, axis), _slab(value, (3 - core) * n, n, axis)], axis
    ).astype(jnp.bfloat16)
    kept = jnp.concatenate([_slab(value, core * n, n, axis), _slab(value, (2 + core) * n, n, axis)], axis)
    half = kept.astype(jnp.float32) + _exchange(sent, 1).astype(jnp.float32)
    sent = _slab(half, (1 - high) * n, n, axis).astype(jnp.bfloat16)
    kept = _slab(half, high * n, n, axis)
    return kept + _exchange(sent, 2).astype(jnp.float32)


def _all_gather(value, axis):
    t = lax.axis_index("tensor")
    core = t % 2
    high = t // 2
    n = value.shape[axis]
    shape = list(value.shape)
    shape[axis] = 2 * n
    pair = jnp.zeros(shape, value.dtype)
    pair = lax.dynamic_update_slice_in_dim(pair, value, high * n, axis)
    pair = lax.dynamic_update_slice_in_dim(pair, _exchange(value, 2), (1 - high) * n, axis)
    other = _exchange(pair, 1)
    shape[axis] = 4 * n
    full = jnp.zeros(shape, value.dtype)
    for part, side in ((pair, core), (other, 1 - core)):
        for a in range(2):
            full = lax.dynamic_update_slice_in_dim(full, _slab(part, a * n, n, axis), (2 * a + side) * n, axis)
    return full


def _exchange_rows(value):
    experts, slots, features = value.shape
    lanes = features
    while lanes > 128 and (slots * features // lanes) % 8 != 0:
        lanes //= 2
    packed = value.reshape(experts, slots * features // lanes, lanes)
    moved = lax.all_to_all(packed, "expert", split_axis=0, concat_axis=0, tiled=True)
    return moved.reshape(experts, slots, features)


def _psum(value):
    value = value + _exchange(value, 1)
    return value + _exchange(value, 2)


def body(attn_partial, residual, norm_gain, expert_ids, route_weight, w_in, w_down):
    token_count = expert_ids.shape[0]
    topk_count = expert_ids.shape[1]
    feature_local = residual.shape[1]
    feature_count = feature_local * lax.axis_size("tensor")
    hidden_width = w_down.shape[1]
    expert_count = lax.axis_size("expert")
    capacity = 5 * token_count * topk_count // (4 * expert_count)
    attention = _reduce_scatter(attn_partial[0], 1)
    stream = residual.astype(jnp.float32) + attention
    squares = _psum(jnp.sum(stream * stream, axis=1))
    inverse = lax.rsqrt(squares / feature_count + 1e-06)[:, None]
    normed = stream * inverse * norm_gain[None, :]
    rows = normed.astype(jnp.bfloat16)
    flat_ids = expert_ids.reshape(-1)
    one_hot = (flat_ids[:, None] == jnp.arange(expert_count, dtype=jnp.int32)[None, :]).astype(
        jnp.int32
    )
    earlier = jnp.cumsum(one_hot, axis=0) - one_hot
    slot_index = jnp.sum(earlier * one_hot, axis=1)
    positions = (flat_ids * capacity + slot_index).reshape(token_count, topk_count)
    places = jnp.arange(expert_count * capacity, dtype=jnp.int32)
    matches = positions[None, :, :] == places[:, None, None]
    dispatch = jnp.any(matches, axis=2)
    sent_rows = jnp.dot(dispatch.astype(jnp.bfloat16), rows, preferred_element_type=jnp.float32)
    sent_rows = sent_rows.astype(jnp.bfloat16).reshape(expert_count, capacity, feature_local)
    weights_table = jnp.sum(jnp.where(matches, route_weight[None, :, :], 0.0), axis=2).T
    in_rows = _exchange_rows(sent_rows)
    source_count = in_rows.shape[0]
    item_count = in_rows.shape[1]
    row_total = source_count * item_count
    flat_rows = in_rows.reshape(row_total, feature_local)
    chunks = 2
    width = hidden_width // chunks
    produced = None
    for j in range(chunks):
        gate = jnp.dot(flat_rows, w_in[0][:, j * width:(j + 1) * width], preferred_element_type=jnp.float32)
        up = jnp.dot(
            flat_rows,
            w_in[0][:, hidden_width + j * width:hidden_width + (j + 1) * width],
            preferred_element_type=jnp.float32,
        )
        partial_value = jnp.concatenate([gate, up], axis=1)
        total = _reduce_scatter(partial_value.astype(jnp.bfloat16), 0)
        hidden = (jax.nn.silu(total[:, :width]) * total[:, width:]).astype(jnp.bfloat16)
        hidden = _all_gather(hidden, 0)
        part = jnp.dot(hidden, w_down[0][j * width:(j + 1) * width, :], preferred_element_type=jnp.float32)
        produced = part if produced is None else produced + part
    produced = produced.astype(jnp.bfloat16)
    results = produced.reshape(source_count, item_count, feature_local)
    returned = _exchange_rows(results)
    routed = jnp.dot(
        weights_table,
        returned.reshape(expert_count * capacity, feature_local).astype(jnp.float32),
        precision=lax.Precision.HIGHEST,
    )
    return (stream + routed).astype(jnp.bfloat16)


def solution(mesh):
    in_specs = (
        P("tensor", "expert", None),
        P("expert", "tensor"),
        P("tensor"),
        P("expert", None),
        P("expert", None),
        P("expert", "tensor", None),
        P("expert", None, "tensor"),
    )
    out_specs = P("expert", "tensor")
    return jax.shard_map(body, mesh=mesh, in_specs=in_specs, out_specs=out_specs, check_vma=False)
```

```python
import jax
import jax.numpy as jnp
from jax import lax
from jax.sharding import PartitionSpec as P


def _exchange(value, flip):
    size = lax.axis_size("tensor")
    return lax.ppermute(value, "tensor", [(j, j ^ flip) for j in range(size)])


def _pick(value, axis, index):
    return lax.dynamic_index_in_dim(value, index, axis=axis, keepdims=False)


def _slab(value, start, size, axis):
    return lax.dynamic_slice_in_dim(value, start, size, axis=axis)


def _reduce_scatter(value, axis):
    t = lax.axis_index("tensor")
    core = t % 2
    high = t // 2
    n = value.shape[axis] // 4
    sent = jnp.concatenate(
        [_slab(value, (1 - core) * n, n, axis), _slab(value, (3 - core) * n, n, axis)], axis
    ).astype(jnp.bfloat16)
    kept = jnp.concatenate([_slab(value, core * n, n, axis), _slab(value, (2 + core) * n, n, axis)], axis)
    half = kept.astype(jnp.float32) + _exchange(sent, 1).astype(jnp.float32)
    sent = _slab(half, (1 - high) * n, n, axis).astype(jnp.bfloat16)
    kept = _slab(half, high * n, n, axis)
    return kept + _exchange(sent, 2).astype(jnp.float32)


def _all_gather(value, axis):
    t = lax.axis_index("tensor")
    core = t % 2
    high = t // 2
    n = value.shape[axis]
    shape = list(value.shape)
    shape[axis] = 2 * n
    pair = jnp.zeros(shape, value.dtype)
    pair = lax.dynamic_update_slice_in_dim(pair, value, high * n, axis)
    pair = lax.dynamic_update_slice_in_dim(pair, _exchange(value, 2), (1 - high) * n, axis)
    other = _exchange(pair, 1)
    shape[axis] = 4 * n
    full = jnp.zeros(shape, value.dtype)
    for part, side in ((pair, core), (other, 1 - core)):
        for a in range(2):
            full = lax.dynamic_update_slice_in_dim(full, _slab(part, a * n, n, axis), (2 * a + side) * n, axis)
    return full


def _exchange_rows(value):
    experts, slots, features = value.shape
    lanes = features
    while lanes > 128 and (slots * features // lanes) % 8 != 0:
        lanes //= 2
    packed = value.reshape(experts, slots * features // lanes, lanes)
    moved = lax.all_to_all(packed, "expert", split_axis=0, concat_axis=0, tiled=True)
    return moved.reshape(experts, slots, features)


def _psum(value):
    value = value + _exchange(value, 1)
    return value + _exchange(value, 2)


def body(attn_partial, residual, norm_gain, expert_ids, route_weight, w_in, w_down):
    token_count = expert_ids.shape[0]
    topk_count = expert_ids.shape[1]
    feature_local = residual.shape[1]
    feature_count = feature_local * lax.axis_size("tensor")
    hidden_width = w_down.shape[1]
    expert_count = lax.axis_size("expert")
    capacity = 5 * token_count * topk_count // (4 * expert_count)
    attention = _reduce_scatter(attn_partial[0], 1)
    stream = residual.astype(jnp.float32) + attention
    squares = _psum(jnp.sum(stream * stream, axis=1))
    inverse = lax.rsqrt(squares / feature_count + 1e-06)[:, None]
    normed = stream * inverse * norm_gain[None, :]
    rows = normed.astype(jnp.bfloat16)
    flat_ids = expert_ids.reshape(-1)
    one_hot = (flat_ids[:, None] == jnp.arange(expert_count, dtype=jnp.int32)[None, :]).astype(
        jnp.int32
    )
    earlier = jnp.cumsum(one_hot, axis=0) - one_hot
    slot_index = jnp.sum(earlier * one_hot, axis=1)
    positions = (flat_ids * capacity + slot_index).reshape(token_count, topk_count)
    places = jnp.arange(expert_count * capacity, dtype=jnp.int32)
    matches = positions[None, :, :] == places[:, None, None]
    dispatch = jnp.any(matches, axis=2)
    sent_rows = jnp.dot(dispatch.astype(jnp.bfloat16), rows, preferred_element_type=jnp.float32)
    sent_rows = sent_rows.astype(jnp.bfloat16).reshape(expert_count, capacity, feature_local)
    weights_table = jnp.sum(jnp.where(matches, route_weight[None, :, :], 0.0), axis=2).T
    in_rows = _exchange_rows(sent_rows)
    source_count = in_rows.shape[0]
    item_count = in_rows.shape[1]
    row_total = source_count * item_count
    flat_rows = in_rows.reshape(row_total, feature_local)
    t = lax.axis_index("tensor")
    core = t % 2
    high = t // 2
    block = row_total // 4
    away = jnp.concatenate(
        [_slab(flat_rows, (1 - core) * block, block, 0), _slab(flat_rows, (3 - core) * block, block, 0)], 0
    )
    home = jnp.concatenate([_slab(flat_rows, core * block, block, 0), _slab(flat_rows, (2 + core) * block, block, 0)], 0)
    sent = jnp.dot(away, w_in[0], preferred_element_type=jnp.float32).astype(jnp.bfloat16)
    received = _exchange(sent, 1)
    kept = jnp.dot(home, w_in[0], preferred_element_type=jnp.float32).astype(jnp.bfloat16)
    half = kept.astype(jnp.float32) + received.astype(jnp.float32)
    sent = _slab(half, (1 - high) * block, block, 0).astype(jnp.bfloat16)
    total = _slab(half, high * block, block, 0) + _exchange(sent, 2).astype(jnp.float32)
    hidden = (jax.nn.silu(total[:, :hidden_width]) * total[:, hidden_width:]).astype(jnp.bfloat16)
    hidden = _all_gather(hidden, 0)
    produced = jnp.dot(hidden, w_down[0], preferred_element_type=jnp.float32).astype(jnp.bfloat16)
    results = produced.reshape(source_count, item_count, feature_local)
    returned = _exchange_rows(results)
    flat_returned = returned.reshape(expert_count * capacity, feature_local)
    weights_high = weights_table.astype(jnp.bfloat16)
    weights_low = (weights_table - weights_high.astype(jnp.float32)).astype(jnp.bfloat16)
    routed = jnp.dot(weights_high, flat_returned, preferred_element_type=jnp.float32) + jnp.dot(
        weights_low, flat_returned, preferred_element_type=jnp.float32
    )
    return (stream + routed).astype(jnp.bfloat16)


def solution(mesh):
    in_specs = (
        P("tensor", "expert", None),
        P("expert", "tensor"),
        P("tensor"),
        P("expert", None),
        P("expert", None),
        P("expert", "tensor", None),
        P("expert", None, "tensor"),
    )
    out_specs = P("expert", "tensor")
    return jax.shard_map(body, mesh=mesh, in_specs=in_specs, out_specs=out_specs, check_vma=False)
```

```python
import jax
import jax.numpy as jnp
from jax import lax
from jax.sharding import PartitionSpec as P


def _exchange(value, flip):
    size = lax.axis_size("tensor")
    return lax.ppermute(value, "tensor", [(j, j ^ flip) for j in range(size)])


def _pick(value, axis, index):
    return lax.dynamic_index_in_dim(value, index, axis=axis, keepdims=False)


def _slab(value, start, size, axis):
    return lax.dynamic_slice_in_dim(value, start, size, axis=axis)


def _reduce_scatter(value, axis):
    t = lax.axis_index("tensor")
    core = t % 2
    high = t // 2
    n = value.shape[axis] // 4
    sent = jnp.concatenate(
        [_slab(value, (1 - core) * n, n, axis), _slab(value, (3 - core) * n, n, axis)], axis
    ).astype(jnp.bfloat16)
    received = _exchange(sent, 1)
    away = _slab(value, (3 - 2 * high + core - 1) * n, n, axis).astype(jnp.float32)
    away = away + _slab(received, (1 - high) * n, n, axis).astype(jnp.float32)
    home = _slab(value, (2 * high + core) * n, n, axis).astype(jnp.float32)
    home = home + _slab(received, high * n, n, axis).astype(jnp.float32)
    return home + _exchange(away.astype(jnp.bfloat16), 2).astype(jnp.float32)


def _reduce_scatter_rows(value):
    t = lax.axis_index("tensor")
    core = t % 2
    high = t // 2
    n = value.shape[0] // 4
    received = _exchange(_slab(value, 2 * (1 - core) * n, 2 * n, 0).astype(jnp.bfloat16), 1)
    away = _slab(value, (2 * core + 1 - high) * n, n, 0).astype(jnp.float32)
    away = away + _slab(received, (1 - high) * n, n, 0).astype(jnp.float32)
    home = _slab(value, (2 * core + high) * n, n, 0).astype(jnp.float32)
    home = home + _slab(received, high * n, n, 0).astype(jnp.float32)
    return home + _exchange(away.astype(jnp.bfloat16), 2).astype(jnp.float32)


def _all_gather_rows(value):
    t = lax.axis_index("tensor")
    core = t % 2
    high = t // 2
    n = value.shape[0]
    pair = jnp.zeros((2 * n,) + value.shape[1:], value.dtype)
    pair = lax.dynamic_update_slice_in_dim(pair, value, high * n, 0)
    pair = lax.dynamic_update_slice_in_dim(pair, _exchange(value, 2), (1 - high) * n, 0)
    full = jnp.zeros((4 * n,) + value.shape[1:], value.dtype)
    full = lax.dynamic_update_slice_in_dim(full, pair, 2 * core * n, 0)
    return lax.dynamic_update_slice_in_dim(full, _exchange(pair, 1), 2 * (1 - core) * n, 0)


def _exchange_rows(value):
    experts, slots, features = value.shape
    lanes = features
    while lanes > 128 and (slots * features // lanes) % 8 != 0:
        lanes //= 2
    packed = value.reshape(experts, slots * features // lanes, lanes)
    moved = lax.all_to_all(packed, "expert", split_axis=0, concat_axis=0, tiled=True)
    return moved.reshape(experts, slots, features)


def _psum(value):
    value = value + _exchange(value, 1)
    return value + _exchange(value, 2)


def body(attn_partial, residual, norm_gain, expert_ids, route_weight, w_in, w_down):
    token_count = expert_ids.shape[0]
    topk_count = expert_ids.shape[1]
    feature_local = residual.shape[1]
    feature_count = feature_local * lax.axis_size("tensor")
    hidden_width = w_down.shape[1]
    expert_count = lax.axis_size("expert")
    capacity = 5 * token_count * topk_count // (4 * expert_count)
    attention = _reduce_scatter(attn_partial[0], 1)
    stream = residual.astype(jnp.float32) + attention
    squares = _psum(jnp.sum(stream * stream, axis=1))
    inverse = lax.rsqrt(squares / feature_count + 1e-06)[:, None]
    normed = stream * inverse * norm_gain[None, :]
    rows = normed.astype(jnp.bfloat16)
    flat_ids = expert_ids.reshape(-1)
    one_hot = (flat_ids[:, None] == jnp.arange(expert_count, dtype=jnp.int32)[None, :]).astype(
        jnp.int32
    )
    earlier = jnp.cumsum(one_hot, axis=0) - one_hot
    slot_index = jnp.sum(earlier * one_hot, axis=1)
    positions = (flat_ids * capacity + slot_index).reshape(token_count, topk_count)
    places = jnp.arange(expert_count * capacity, dtype=jnp.int32)
    matches = positions[None, :, :] == places[:, None, None]
    dispatch = jnp.any(matches, axis=2)
    sent_rows = jnp.dot(dispatch.astype(jnp.bfloat16), rows, preferred_element_type=jnp.float32)
    sent_rows = sent_rows.astype(jnp.bfloat16).reshape(expert_count, capacity, feature_local)
    weights_table = jnp.sum(jnp.where(matches, route_weight[None, :, :], 0.0), axis=2).T
    in_rows = _exchange_rows(sent_rows)
    source_count = in_rows.shape[0]
    item_count = in_rows.shape[1]
    row_total = source_count * item_count
    flat_rows = in_rows.reshape(row_total, feature_local)
    partial_value = jnp.dot(flat_rows, w_in[0], preferred_element_type=jnp.float32)
    total = _reduce_scatter_rows(partial_value.astype(jnp.bfloat16))
    hidden = (jax.nn.silu(total[:, :hidden_width]) * total[:, hidden_width:]).astype(jnp.bfloat16)
    hidden = _all_gather_rows(hidden)
    produced = jnp.dot(hidden, w_down[0], preferred_element_type=jnp.float32).astype(jnp.bfloat16)
    results = produced.reshape(source_count, item_count, feature_local)
    returned = _exchange_rows(results)
    routed = jnp.dot(
        weights_table,
        returned.reshape(expert_count * capacity, feature_local).astype(jnp.float32),
        precision=lax.Precision.HIGHEST,
    )
    return (stream + routed).astype(jnp.bfloat16)


def solution(mesh):
    in_specs = (
        P("tensor", "expert", None),
        P("expert", "tensor"),
        P("tensor"),
        P("expert", None),
        P("expert", None),
        P("expert", "tensor", None),
        P("expert", None, "tensor"),
    )
    out_specs = P("expert", "tensor")
    return jax.shard_map(body, mesh=mesh, in_specs=in_specs, out_specs=out_specs, check_vma=False)
```

```python
import jax
import jax.numpy as jnp
from jax import lax
from jax.sharding import PartitionSpec as P


def _exchange(value, flip):
    size = lax.axis_size("tensor")
    return lax.ppermute(value, "tensor", [(j, j ^ flip) for j in range(size)])


def _slab(value, start, size, axis):
    return lax.dynamic_slice_in_dim(value, start, size, axis=axis)


def _reduce_scatter(value, axis):
    t = lax.axis_index("tensor")
    core = t % 2
    high = t // 2
    n = value.shape[axis] // 4
    sent = jnp.concatenate(
        [_slab(value, (1 - core) * n, n, axis), _slab(value, (3 - core) * n, n, axis)], axis
    ).astype(jnp.bfloat16)
    received = _exchange(sent, 1)
    away = _slab(value, (3 - 2 * high + core - 1) * n, n, axis).astype(jnp.float32)
    away = away + _slab(received, (1 - high) * n, n, axis).astype(jnp.float32)
    home = _slab(value, (2 * high + core) * n, n, axis).astype(jnp.float32)
    home = home + _slab(received, high * n, n, axis).astype(jnp.float32)
    return home + _exchange(away.astype(jnp.bfloat16), 2).astype(jnp.float32)


def _all_gather_rows(value):
    t = lax.axis_index("tensor")
    core = t % 2
    high = t // 2
    n = value.shape[0]
    pair = jnp.zeros((2 * n,) + value.shape[1:], value.dtype)
    pair = lax.dynamic_update_slice_in_dim(pair, value, high * n, 0)
    pair = lax.dynamic_update_slice_in_dim(pair, _exchange(value, 2), (1 - high) * n, 0)
    full = jnp.zeros((4 * n,) + value.shape[1:], value.dtype)
    full = lax.dynamic_update_slice_in_dim(full, pair, 2 * core * n, 0)
    return lax.dynamic_update_slice_in_dim(full, _exchange(pair, 1), 2 * (1 - core) * n, 0)


def _exchange_rows(value):
    experts, slots, features = value.shape
    lanes = features
    while lanes > 128 and (slots * features // lanes) % 8 != 0:
        lanes //= 2
    packed = value.reshape(experts, slots * features // lanes, lanes)
    moved = lax.all_to_all(packed, "expert", split_axis=0, concat_axis=0, tiled=True)
    return moved.reshape(experts, slots, features)


def _psum(value):
    value = value + _exchange(value, 1)
    return value + _exchange(value, 2)


def _body(attn_partial, residual, norm_gain, expert_ids, route_weight, w_in, w_down):
    token_count = expert_ids.shape[0]
    topk_count = expert_ids.shape[1]
    feature_local = residual.shape[1]
    feature_count = feature_local * lax.axis_size("tensor")
    hidden_width = w_down.shape[1]
    expert_count = lax.axis_size("expert")
    capacity = 5 * token_count * topk_count // (4 * expert_count)
    attention = _reduce_scatter(attn_partial[0], 1)
    stream = residual.astype(jnp.float32) + attention
    squares = _psum(jnp.sum(stream * stream, axis=1))
    inverse = lax.rsqrt(squares / feature_count + 1e-06)[:, None]
    normed = stream * inverse * norm_gain[None, :]
    rows = normed.astype(jnp.bfloat16)
    flat_ids = expert_ids.reshape(-1)
    one_hot = (flat_ids[:, None] == jnp.arange(expert_count, dtype=jnp.int32)[None, :]).astype(
        jnp.int32
    )
    earlier = jnp.cumsum(one_hot, axis=0) - one_hot
    slot_index = jnp.sum(earlier * one_hot, axis=1)
    positions = (flat_ids * capacity + slot_index).reshape(token_count, topk_count)
    places = jnp.arange(expert_count * capacity, dtype=jnp.int32)
    matches = positions[None, :, :] == places[:, None, None]
    dispatch = jnp.any(matches, axis=2)
    sent_rows = jnp.dot(dispatch.astype(jnp.bfloat16), rows, preferred_element_type=jnp.float32)
    sent_rows = sent_rows.astype(jnp.bfloat16).reshape(expert_count, capacity, feature_local)
    weights_table = jnp.sum(jnp.where(matches, route_weight[None, :, :], 0.0), axis=2).T
    in_rows = _exchange_rows(sent_rows)
    source_count = in_rows.shape[0]
    item_count = in_rows.shape[1]
    row_total = source_count * item_count
    flat_rows = in_rows.reshape(row_total, feature_local)
    t = lax.axis_index("tensor")
    core = t % 2
    high = t // 2
    block = row_total // 4
    away_rows = _slab(flat_rows, 2 * (1 - core) * block, 2 * block, 0)
    home_rows = _slab(flat_rows, 2 * core * block, 2 * block, 0)
    sent = jnp.dot(away_rows, w_in[0], preferred_element_type=jnp.float32).astype(jnp.bfloat16)
    home_rows, sent = lax.optimization_barrier((home_rows, sent))
    received = _exchange(sent, 1)
    kept = jnp.dot(home_rows, w_in[0], preferred_element_type=jnp.float32).astype(jnp.bfloat16)
    away = _slab(kept, (1 - high) * block, block, 0).astype(jnp.float32)
    away = away + _slab(received, (1 - high) * block, block, 0).astype(jnp.float32)
    far = _exchange(away.astype(jnp.bfloat16), 2)
    home = _slab(kept, high * block, block, 0).astype(jnp.float32)
    home = lax.optimization_barrier(home + _slab(received, high * block, block, 0).astype(jnp.float32))
    total = home + far.astype(jnp.float32)
    hidden = (jax.nn.silu(total[:, :hidden_width]) * total[:, hidden_width:]).astype(jnp.bfloat16)
    hidden = _all_gather_rows(hidden)
    produced = jnp.dot(hidden, w_down[0], preferred_element_type=jnp.float32).astype(jnp.bfloat16)
    results = produced.reshape(source_count, item_count, feature_local)
    returned = _exchange_rows(results)
    routed = jnp.dot(
        weights_table,
        returned.reshape(expert_count * capacity, feature_local).astype(jnp.float32),
        precision=lax.Precision.HIGHEST,
    )
    return (stream + routed).astype(jnp.bfloat16)


def solution(mesh):
    in_specs = (
        P("tensor", "expert", None),
        P("expert", "tensor"),
        P("tensor"),
        P("expert", None),
        P("expert", None),
        P("expert", "tensor", None),
        P("expert", None, "tensor"),
    )
    out_specs = P("expert", "tensor")
    return jax.shard_map(_body, mesh=mesh, in_specs=in_specs, out_specs=out_specs, check_vma=False)
```

```python
import jax
import jax.numpy as jnp
from jax import lax
from jax.sharding import PartitionSpec as P


def _exchange(value, flip):
    size = lax.axis_size("tensor")
    return lax.ppermute(value, "tensor", [(j, j ^ flip) for j in range(size)])


def _slab(value, start, size, axis):
    return lax.dynamic_slice_in_dim(value, start, size, axis=axis)


def _reduce_scatter(value, axis):
    t = lax.axis_index("tensor")
    core = t % 2
    high = t // 2
    n = value.shape[axis] // 4
    sent = jnp.concatenate(
        [_slab(value, (1 - core) * n, n, axis), _slab(value, (3 - core) * n, n, axis)], axis
    ).astype(jnp.bfloat16)
    received = _exchange(sent, 1)
    away = _slab(value, (3 - 2 * high + core - 1) * n, n, axis).astype(jnp.float32)
    away = away + _slab(received, (1 - high) * n, n, axis).astype(jnp.float32)
    far = _exchange(away.astype(jnp.bfloat16), 2)
    home = _slab(value, (2 * high + core) * n, n, axis).astype(jnp.float32)
    home = lax.optimization_barrier(home + _slab(received, high * n, n, axis).astype(jnp.float32))
    return home + far.astype(jnp.float32)


def _all_gather_rows(value):
    t = lax.axis_index("tensor")
    core = t % 2
    high = t // 2
    n = value.shape[0]
    pair = jnp.zeros((2 * n,) + value.shape[1:], value.dtype)
    pair = lax.dynamic_update_slice_in_dim(pair, value, high * n, 0)
    pair = lax.dynamic_update_slice_in_dim(pair, _exchange(value, 2), (1 - high) * n, 0)
    full = jnp.zeros((4 * n,) + value.shape[1:], value.dtype)
    full = lax.dynamic_update_slice_in_dim(full, pair, 2 * core * n, 0)
    return lax.dynamic_update_slice_in_dim(full, _exchange(pair, 1), 2 * (1 - core) * n, 0)


def _exchange_rows(value):
    experts, slots, features = value.shape
    lanes = features
    while lanes > 128 and (slots * features // lanes) % 8 != 0:
        lanes //= 2
    packed = value.reshape(experts, slots * features // lanes, lanes)
    moved = lax.all_to_all(packed, "expert", split_axis=0, concat_axis=0, tiled=True)
    return moved.reshape(experts, slots, features)


def _psum(value):
    value = value + _exchange(value, 1)
    return value + _exchange(value, 2)


def _body(attn_partial, residual, norm_gain, expert_ids, route_weight, w_in, w_down):
    token_count = expert_ids.shape[0]
    topk_count = expert_ids.shape[1]
    feature_local = residual.shape[1]
    feature_count = feature_local * lax.axis_size("tensor")
    hidden_width = w_down.shape[1]
    expert_count = lax.axis_size("expert")
    capacity = 5 * token_count * topk_count // (4 * expert_count)
    attention = _reduce_scatter(attn_partial[0], 1)
    stream = residual.astype(jnp.float32) + attention
    squares = _psum(jnp.sum(stream * stream, axis=1))
    inverse = lax.rsqrt(squares / feature_count + 1e-06)[:, None]
    normed = stream * inverse * norm_gain[None, :]
    rows = normed.astype(jnp.bfloat16)
    flat_ids = expert_ids.reshape(-1)
    one_hot = (flat_ids[:, None] == jnp.arange(expert_count, dtype=jnp.int32)[None, :]).astype(
        jnp.int32
    )
    earlier = jnp.cumsum(one_hot, axis=0) - one_hot
    slot_index = jnp.sum(earlier * one_hot, axis=1)
    positions = (flat_ids * capacity + slot_index).reshape(token_count, topk_count)
    places = jnp.arange(expert_count * capacity, dtype=jnp.int32)
    matches = positions[None, :, :] == places[:, None, None]
    dispatch = jnp.any(matches, axis=2)
    sent_rows = jnp.dot(dispatch.astype(jnp.bfloat16), rows, preferred_element_type=jnp.float32)
    sent_rows = sent_rows.astype(jnp.bfloat16).reshape(expert_count, capacity, feature_local)
    weights_table = jnp.sum(jnp.where(matches, route_weight[None, :, :], 0.0), axis=2).T
    in_rows = _exchange_rows(sent_rows)
    source_count = in_rows.shape[0]
    item_count = in_rows.shape[1]
    row_total = source_count * item_count
    flat_rows = in_rows.reshape(row_total, feature_local)
    t = lax.axis_index("tensor")
    core = t % 2
    high = t // 2
    block = row_total // 4
    away_rows = _slab(flat_rows, 2 * (1 - core) * block, 2 * block, 0)
    home_rows = _slab(flat_rows, 2 * core * block, 2 * block, 0)
    sent = jnp.dot(away_rows, w_in[0], preferred_element_type=jnp.float32).astype(jnp.bfloat16)
    home_rows, sent = lax.optimization_barrier((home_rows, sent))
    received = _exchange(sent, 1)
    kept = jnp.dot(home_rows, w_in[0], preferred_element_type=jnp.float32).astype(jnp.bfloat16)
    away = _slab(kept, (1 - high) * block, block, 0).astype(jnp.float32)
    away = away + _slab(received, (1 - high) * block, block, 0).astype(jnp.float32)
    far = _exchange(away.astype(jnp.bfloat16), 2)
    home = _slab(kept, high * block, block, 0).astype(jnp.float32)
    home = lax.optimization_barrier(home + _slab(received, high * block, block, 0).astype(jnp.float32))
    total = home + far.astype(jnp.float32)
    hidden = (jax.nn.silu(total[:, :hidden_width]) * total[:, hidden_width:]).astype(jnp.bfloat16)
    hidden = _all_gather_rows(hidden)
    produced = jnp.dot(hidden, w_down[0], preferred_element_type=jnp.float32).astype(jnp.bfloat16)
    results = produced.reshape(source_count, item_count, feature_local)
    returned = _exchange_rows(results)
    flat_returned = returned.reshape(expert_count * capacity, feature_local)
    weights_high = weights_table.astype(jnp.bfloat16)
    weights_low = (weights_table - weights_high.astype(jnp.float32)).astype(jnp.bfloat16)
    both = jnp.dot(
        jnp.concatenate([weights_high, weights_low], 0), flat_returned, preferred_element_type=jnp.float32
    )
    routed = both[:token_count] + both[token_count:]
    return (stream + routed).astype(jnp.bfloat16)


def solution(mesh):
    in_specs = (
        P("tensor", "expert", None),
        P("expert", "tensor"),
        P("tensor"),
        P("expert", None),
        P("expert", None),
        P("expert", "tensor", None),
        P("expert", None, "tensor"),
    )
    out_specs = P("expert", "tensor")
    return jax.shard_map(_body, mesh=mesh, in_specs=in_specs, out_specs=out_specs, check_vma=False)
```

```python
import jax
import jax.numpy as jnp
from jax import lax
from jax.sharding import PartitionSpec as P


def _exchange(value, flip):
    size = lax.axis_size("tensor")
    return lax.ppermute(value, "tensor", [(j, j ^ flip) for j in range(size)])


def _slab(value, start, size, axis):
    return lax.dynamic_slice_in_dim(value, start, size, axis=axis)


def _reduce_scatter(value, axis):
    t = lax.axis_index("tensor")
    core = t % 2
    high = t // 2
    n = value.shape[axis] // 4
    sent = jnp.concatenate(
        [_slab(value, (1 - core) * n, n, axis), _slab(value, (3 - core) * n, n, axis)], axis
    ).astype(jnp.bfloat16)
    received = _exchange(sent, 1)
    away = _slab(value, (3 - 2 * high + core - 1) * n, n, axis).astype(jnp.float32)
    away = away + _slab(received, (1 - high) * n, n, axis).astype(jnp.float32)
    far = _exchange(away.astype(jnp.bfloat16), 2)
    home = _slab(value, (2 * high + core) * n, n, axis).astype(jnp.float32)
    home = lax.optimization_barrier(home + _slab(received, high * n, n, axis).astype(jnp.float32))
    return home + far.astype(jnp.float32)


def _all_gather_rows(value):
    t = lax.axis_index("tensor")
    core = t % 2
    high = t // 2
    n = value.shape[0]
    pair = jnp.zeros((2 * n,) + value.shape[1:], value.dtype)
    pair = lax.dynamic_update_slice_in_dim(pair, value, high * n, 0)
    pair = lax.dynamic_update_slice_in_dim(pair, _exchange(value, 2), (1 - high) * n, 0)
    full = jnp.zeros((4 * n,) + value.shape[1:], value.dtype)
    full = lax.dynamic_update_slice_in_dim(full, pair, 2 * core * n, 0)
    return lax.dynamic_update_slice_in_dim(full, _exchange(pair, 1), 2 * (1 - core) * n, 0)


def _exchange_rows(value):
    experts, slots, features = value.shape
    lanes = features
    while lanes > 128 and (slots * features // lanes) % 8 != 0:
        lanes //= 2
    packed = value.reshape(experts, slots * features // lanes, lanes)
    moved = lax.all_to_all(packed, "expert", split_axis=0, concat_axis=0, tiled=True)
    return moved.reshape(experts, slots, features)


def _psum(value):
    value = value + _exchange(value, 1)
    return value + _exchange(value, 2)


def _body(attn_partial, residual, norm_gain, expert_ids, route_weight, w_in, w_down):
    token_count = expert_ids.shape[0]
    topk_count = expert_ids.shape[1]
    feature_local = residual.shape[1]
    feature_count = feature_local * lax.axis_size("tensor")
    hidden_width = w_down.shape[1]
    expert_count = lax.axis_size("expert")
    capacity = 5 * token_count * topk_count // (4 * expert_count)
    attention = _reduce_scatter(attn_partial[0], 1)
    stream = residual.astype(jnp.float32) + attention
    squares = _psum(jnp.sum(stream * stream, axis=1))
    inverse = lax.rsqrt(squares / feature_count + 1e-06)[:, None]
    normed = stream * inverse * norm_gain[None, :]
    rows = normed.astype(jnp.bfloat16)
    flat_ids = expert_ids.reshape(-1)
    one_hot = (flat_ids[:, None] == jnp.arange(expert_count, dtype=jnp.int32)[None, :]).astype(
        jnp.int32
    )
    earlier = jnp.cumsum(one_hot, axis=0) - one_hot
    slot_index = jnp.sum(earlier * one_hot, axis=1)
    positions = (flat_ids * capacity + slot_index).reshape(token_count, topk_count)
    places = jnp.arange(expert_count * capacity, dtype=jnp.int32)
    matches = positions[None, :, :] == places[:, None, None]
    dispatch = jnp.any(matches, axis=2)
    sent_rows = jnp.dot(dispatch.astype(jnp.bfloat16), rows, preferred_element_type=jnp.float32)
    sent_rows = sent_rows.astype(jnp.bfloat16).reshape(expert_count, capacity, feature_local)
    weights_table = jnp.sum(jnp.where(matches, route_weight[None, :, :], 0.0), axis=2).T
    in_rows = _exchange_rows(sent_rows)
    source_count = in_rows.shape[0]
    item_count = in_rows.shape[1]
    row_total = source_count * item_count
    flat_rows = in_rows.reshape(row_total, feature_local)
    t = lax.axis_index("tensor")
    core = t % 2
    high = t // 2
    block = row_total // 4
    away_rows = _slab(flat_rows, 2 * (1 - core) * block, 2 * block, 0)
    home_rows = _slab(flat_rows, 2 * core * block, 2 * block, 0)
    sent = jnp.dot(away_rows, w_in[0], preferred_element_type=jnp.float32).astype(jnp.bfloat16)
    home_rows, sent = lax.optimization_barrier((home_rows, sent))
    received = _exchange(sent, 1)
    kept = jnp.dot(home_rows, w_in[0], preferred_element_type=jnp.float32).astype(jnp.bfloat16)
    away = _slab(kept, (1 - high) * block, block, 0).astype(jnp.float32)
    away = away + _slab(received, (1 - high) * block, block, 0).astype(jnp.float32)
    far = _exchange(away.astype(jnp.bfloat16), 2)
    home = _slab(kept, high * block, block, 0).astype(jnp.float32)
    home = lax.optimization_barrier(home + _slab(received, high * block, block, 0).astype(jnp.float32))
    total = home + far.astype(jnp.float32)
    hidden = (jax.nn.silu(total[:, :hidden_width]) * total[:, hidden_width:]).astype(jnp.bfloat16)
    hidden = _all_gather_rows(hidden)
    produced = jnp.dot(hidden, w_down[0], preferred_element_type=jnp.float32).astype(jnp.bfloat16)
    results = produced.reshape(source_count, item_count, feature_local)
    returned = _exchange_rows(results)
    routed = jnp.dot(
        weights_table,
        returned.reshape(expert_count * capacity, feature_local).astype(jnp.float32),
        precision=lax.Precision.HIGHEST,
    )
    return (stream + routed).astype(jnp.bfloat16)


def solution(mesh):
    in_specs = (
        P("tensor", "expert", None),
        P("expert", "tensor"),
        P("tensor"),
        P("expert", None),
        P("expert", None),
        P("expert", "tensor", None),
        P("expert", None, "tensor"),
    )
    out_specs = P("expert", "tensor")
    return jax.shard_map(_body, mesh=mesh, in_specs=in_specs, out_specs=out_specs, check_vma=False)
```

```python
import jax
import jax.numpy as jnp
from jax import lax
from jax.sharding import PartitionSpec as P


def _exchange(value, flip):
    size = lax.axis_size("tensor")
    return lax.ppermute(value, "tensor", [(j, j ^ flip) for j in range(size)])


def _slab(value, start, size, axis):
    return lax.dynamic_slice_in_dim(value, start, size, axis=axis)


def _reduce_scatter(value, axis):
    t = lax.axis_index("tensor")
    core = t % 2
    high = t // 2
    n = value.shape[axis] // 4
    sent = jnp.concatenate(
        [_slab(value, (1 - core) * n, n, axis), _slab(value, (3 - core) * n, n, axis)], axis
    ).astype(jnp.bfloat16)
    received = _exchange(sent, 1)
    away = _slab(value, (3 - 2 * high + core - 1) * n, n, axis).astype(jnp.float32)
    away = away + _slab(received, (1 - high) * n, n, axis).astype(jnp.float32)
    home = _slab(value, (2 * high + core) * n, n, axis).astype(jnp.float32)
    home = home + _slab(received, high * n, n, axis).astype(jnp.float32)
    return home + _exchange(away.astype(jnp.bfloat16), 2).astype(jnp.float32)


def _all_gather_rows(value):
    t = lax.axis_index("tensor")
    core = t % 2
    high = t // 2
    n = value.shape[0]
    pair = jnp.zeros((2 * n,) + value.shape[1:], value.dtype)
    pair = lax.dynamic_update_slice_in_dim(pair, value, high * n, 0)
    pair = lax.dynamic_update_slice_in_dim(pair, _exchange(value, 2), (1 - high) * n, 0)
    full = jnp.zeros((4 * n,) + value.shape[1:], value.dtype)
    full = lax.dynamic_update_slice_in_dim(full, pair, 2 * core * n, 0)
    return lax.dynamic_update_slice_in_dim(full, _exchange(pair, 1), 2 * (1 - core) * n, 0)


def _exchange_rows(value):
    experts, slots, features = value.shape
    lanes = 128
    packed = value.reshape(experts, slots * features // lanes, lanes)
    return lax.all_to_all(packed, "expert", split_axis=0, concat_axis=0, tiled=True)


def _psum(value):
    value = value + _exchange(value, 1)
    return value + _exchange(value, 2)


def _body(attn_partial, residual, norm_gain, expert_ids, route_weight, w_in, w_down):
    token_count = expert_ids.shape[0]
    topk_count = expert_ids.shape[1]
    feature_local = residual.shape[1]
    feature_count = feature_local * lax.axis_size("tensor")
    hidden_width = w_down.shape[1]
    expert_count = lax.axis_size("expert")
    capacity = 5 * token_count * topk_count // (4 * expert_count)
    attention = _reduce_scatter(attn_partial[0], 1)
    stream = residual.astype(jnp.float32) + attention
    squares = _psum(jnp.sum(stream * stream, axis=1))
    inverse = lax.rsqrt(squares / feature_count + 1e-06)[:, None]
    normed = stream * inverse * norm_gain[None, :]
    rows = normed.astype(jnp.bfloat16)
    flat_ids = expert_ids.reshape(-1)
    one_hot = (flat_ids[:, None] == jnp.arange(expert_count, dtype=jnp.int32)[None, :]).astype(
        jnp.int32
    )
    earlier = jnp.cumsum(one_hot, axis=0) - one_hot
    slot_index = jnp.sum(earlier * one_hot, axis=1)
    positions = (flat_ids * capacity + slot_index).reshape(token_count, topk_count)
    places = jnp.arange(expert_count * capacity, dtype=jnp.int32)
    matches = positions[None, :, :] == places[:, None, None]
    dispatch = jnp.any(matches, axis=2)
    sent_rows = jnp.dot(dispatch.astype(jnp.bfloat16), rows, preferred_element_type=jnp.float32)
    sent_rows = sent_rows.astype(jnp.bfloat16).reshape(expert_count, capacity, feature_local)
    weights_table = jnp.sum(jnp.where(matches, route_weight[None, :, :], 0.0), axis=2).T
    in_rows = _exchange_rows(sent_rows)
    source_count = sent_rows.shape[0]
    item_count = sent_rows.shape[1]
    row_total = source_count * item_count
    t = lax.axis_index("tensor")
    core = t % 2
    high = t // 2
    block = row_total // 4
    sources = source_count // 2
    away_rows = _slab(in_rows, (1 - core) * sources, sources, 0).reshape(2 * block, feature_local)
    sent = jnp.dot(away_rows, w_in[0], preferred_element_type=jnp.float32).astype(jnp.bfloat16)
    in_rows, sent = lax.optimization_barrier((in_rows, sent))
    received = _exchange(sent, 1)
    home_rows = _slab(in_rows, core * sources, sources, 0).reshape(2 * block, feature_local)
    kept = jnp.dot(home_rows, w_in[0], preferred_element_type=jnp.float32).astype(jnp.bfloat16)
    away = _slab(kept, (1 - high) * block, block, 0).astype(jnp.float32)
    away = away + _slab(received, (1 - high) * block, block, 0).astype(jnp.float32)
    far = _exchange(away.astype(jnp.bfloat16), 2)
    home = _slab(kept, high * block, block, 0).astype(jnp.float32)
    home = lax.optimization_barrier(home + _slab(received, high * block, block, 0).astype(jnp.float32))
    total = home + far.astype(jnp.float32)
    hidden = (jax.nn.silu(total[:, :hidden_width]) * total[:, hidden_width:]).astype(jnp.bfloat16)
    hidden = _all_gather_rows(hidden)
    produced = jnp.dot(hidden, w_down[0], preferred_element_type=jnp.float32).astype(jnp.bfloat16)
    results = produced.reshape(source_count, item_count, feature_local)
    returned = _exchange_rows(results).reshape(expert_count, capacity, feature_local)
    routed = jnp.dot(
        weights_table,
        returned.reshape(expert_count * capacity, feature_local).astype(jnp.float32),
        precision=lax.Precision.HIGHEST,
    )
    return (stream + routed).astype(jnp.bfloat16)


def solution(mesh):
    in_specs = (
        P("tensor", "expert", None),
        P("expert", "tensor"),
        P("tensor"),
        P("expert", None),
        P("expert", None),
        P("expert", "tensor", None),
        P("expert", None, "tensor"),
    )
    out_specs = P("expert", "tensor")
    return jax.shard_map(_body, mesh=mesh, in_specs=in_specs, out_specs=out_specs, check_vma=False)
```

```python
import jax
import jax.numpy as jnp
from jax import lax
from jax.sharding import PartitionSpec as P


def _exchange(value, flip):
    size = lax.axis_size("tensor")
    return lax.ppermute(value, "tensor", [(j, j ^ flip) for j in range(size)])


def _slab(value, start, size, axis):
    return lax.dynamic_slice_in_dim(value, start, size, axis=axis)


def _reduce_scatter(value, axis):
    t = lax.axis_index("tensor")
    core = t % 2
    high = t // 2
    n = value.shape[axis] // 4
    first = _exchange(_slab(value, (1 - core) * n, n, axis).astype(jnp.bfloat16), 1)
    second = _exchange(_slab(value, (3 - core) * n, n, axis).astype(jnp.bfloat16), 1)
    away_in, home_in = jnp.where(high == 0, second, first), jnp.where(high == 0, first, second)
    away = _slab(value, (3 - 2 * high + core - 1) * n, n, axis).astype(jnp.float32) + away_in.astype(jnp.float32)
    home = _slab(value, (2 * high + core) * n, n, axis).astype(jnp.float32) + home_in.astype(jnp.float32)
    return home + _exchange(away.astype(jnp.bfloat16), 2).astype(jnp.float32)


def _all_gather_rows(value):
    t = lax.axis_index("tensor")
    core = t % 2
    high = t // 2
    n = value.shape[0]
    pair = jnp.zeros((2 * n,) + value.shape[1:], value.dtype)
    pair = lax.dynamic_update_slice_in_dim(pair, value, high * n, 0)
    pair = lax.dynamic_update_slice_in_dim(pair, _exchange(value, 2), (1 - high) * n, 0)
    full = jnp.zeros((4 * n,) + value.shape[1:], value.dtype)
    full = lax.dynamic_update_slice_in_dim(full, pair, 2 * core * n, 0)
    return lax.dynamic_update_slice_in_dim(full, _exchange(pair, 1), 2 * (1 - core) * n, 0)


def _exchange_rows(value):
    experts, slots, features = value.shape
    lanes = 128
    packed = value.reshape(experts, slots * features // lanes, lanes)
    moved = lax.all_to_all(packed, "expert", split_axis=0, concat_axis=0, tiled=True)
    return moved.reshape(experts, slots, features)


def _psum(value):
    value = value + _exchange(value, 1)
    return value + _exchange(value, 2)


def _body(attn_partial, residual, norm_gain, expert_ids, route_weight, w_in, w_down):
    token_count = expert_ids.shape[0]
    topk_count = expert_ids.shape[1]
    feature_local = residual.shape[1]
    feature_count = feature_local * lax.axis_size("tensor")
    hidden_width = w_down.shape[1]
    expert_count = lax.axis_size("expert")
    capacity = 5 * token_count * topk_count // (4 * expert_count)
    attention = _reduce_scatter(attn_partial[0], 1)
    stream = residual.astype(jnp.float32) + attention
    squares = _psum(jnp.sum(stream * stream, axis=1))
    inverse = lax.rsqrt(squares / feature_count + 1e-06)[:, None]
    normed = stream * inverse * norm_gain[None, :]
    rows = normed.astype(jnp.bfloat16)
    flat_ids = expert_ids.reshape(-1)
    one_hot = (flat_ids[:, None] == jnp.arange(expert_count, dtype=jnp.int32)[None, :]).astype(
        jnp.int32
    )
    earlier = jnp.cumsum(one_hot, axis=0) - one_hot
    slot_index = jnp.sum(earlier * one_hot, axis=1)
    positions = (flat_ids * capacity + slot_index).reshape(token_count, topk_count)
    places = jnp.arange(expert_count * capacity, dtype=jnp.int32)
    matches = positions[None, :, :] == places[:, None, None]
    dispatch = jnp.any(matches, axis=2)
    sent_rows = jnp.dot(dispatch.astype(jnp.bfloat16), rows, preferred_element_type=jnp.float32)
    sent_rows = sent_rows.astype(jnp.bfloat16).reshape(expert_count, capacity, feature_local)
    weights_table = jnp.sum(jnp.where(matches, route_weight[None, :, :], 0.0), axis=2).T
    in_rows = _exchange_rows(sent_rows)
    source_count = in_rows.shape[0]
    item_count = in_rows.shape[1]
    row_total = source_count * item_count
    flat_rows = in_rows.reshape(row_total, feature_local)
    t = lax.axis_index("tensor")
    core = t % 2
    high = t // 2
    block = row_total // 4
    away_rows = _slab(flat_rows, 2 * (1 - core) * block, 2 * block, 0)
    home_rows = _slab(flat_rows, 2 * core * block, 2 * block, 0)
    sent = jnp.dot(away_rows, w_in[0], preferred_element_type=jnp.float32).astype(jnp.bfloat16)
    home_rows, sent = lax.optimization_barrier((home_rows, sent))
    received = _exchange(sent, 1)
    kept = jnp.dot(home_rows, w_in[0], preferred_element_type=jnp.float32).astype(jnp.bfloat16)
    away = _slab(kept, (1 - high) * block, block, 0).astype(jnp.float32)
    away = away + _slab(received, (1 - high) * block, block, 0).astype(jnp.float32)
    far = _exchange(away.astype(jnp.bfloat16), 2)
    home = _slab(kept, high * block, block, 0).astype(jnp.float32)
    home = lax.optimization_barrier(home + _slab(received, high * block, block, 0).astype(jnp.float32))
    total = home + far.astype(jnp.float32)
    hidden = (jax.nn.silu(total[:, :hidden_width]) * total[:, hidden_width:]).astype(jnp.bfloat16)
    hidden = _all_gather_rows(hidden)
    produced = jnp.dot(hidden, w_down[0], preferred_element_type=jnp.float32).astype(jnp.bfloat16)
    results = produced.reshape(source_count, item_count, feature_local)
    returned = _exchange_rows(results)
    routed = jnp.dot(
        weights_table,
        returned.reshape(expert_count * capacity, feature_local).astype(jnp.float32),
        precision=lax.Precision.HIGHEST,
    )
    return (stream + routed).astype(jnp.bfloat16)


def solution(mesh):
    in_specs = (
        P("tensor", "expert", None),
        P("expert", "tensor"),
        P("tensor"),
        P("expert", None),
        P("expert", None),
        P("expert", "tensor", None),
        P("expert", None, "tensor"),
    )
    out_specs = P("expert", "tensor")
    return jax.shard_map(_body, mesh=mesh, in_specs=in_specs, out_specs=out_specs, check_vma=False)
```

```python
import jax
import jax.numpy as jnp
from jax import lax
from jax.sharding import PartitionSpec as P


def _exchange(value, flip):
    size = lax.axis_size("tensor")
    return lax.ppermute(value, "tensor", [(j, j ^ flip) for j in range(size)])


def _slab(value, start, size, axis):
    return lax.dynamic_slice_in_dim(value, start, size, axis=axis)


def _reduce_scatter(value, axis):
    t = lax.axis_index("tensor")
    core = t % 2
    high = t // 2
    n = value.shape[axis] // 4
    sent = jnp.concatenate(
        [_slab(value, (1 - core) * n, n, axis), _slab(value, (3 - core) * n, n, axis)], axis
    ).astype(jnp.bfloat16)
    received = _exchange(sent, 1)
    away = _slab(value, (3 - 2 * high + core - 1) * n, n, axis).astype(jnp.float32)
    away = away + _slab(received, (1 - high) * n, n, axis).astype(jnp.float32)
    home = _slab(value, (2 * high + core) * n, n, axis).astype(jnp.float32)
    home = home + _slab(received, high * n, n, axis).astype(jnp.float32)
    return home + _exchange(away.astype(jnp.bfloat16), 2).astype(jnp.float32)


def _all_gather_rows(value):
    t = lax.axis_index("tensor")
    core = t % 2
    high = t // 2
    n = value.shape[0]
    pair = jnp.zeros((2 * n,) + value.shape[1:], value.dtype)
    pair = lax.dynamic_update_slice_in_dim(pair, value, high * n, 0)
    pair = lax.dynamic_update_slice_in_dim(pair, _exchange(value, 2), (1 - high) * n, 0)
    full = jnp.zeros((4 * n,) + value.shape[1:], value.dtype)
    full = lax.dynamic_update_slice_in_dim(full, pair, 2 * core * n, 0)
    return lax.dynamic_update_slice_in_dim(full, _exchange(pair, 1), 2 * (1 - core) * n, 0)


def _exchange_rows(value):
    experts, slots, features = value.shape
    lanes = 128
    packed = value.reshape(experts, slots * features // lanes, lanes)
    moved = lax.all_to_all(packed, "expert", split_axis=0, concat_axis=0, tiled=True)
    return moved.reshape(experts, slots, features)


def _psum(value):
    value = value + _exchange(value, 1)
    return value + _exchange(value, 2)


def _body(attn_partial, residual, norm_gain, expert_ids, route_weight, w_in, w_down):
    token_count = expert_ids.shape[0]
    topk_count = expert_ids.shape[1]
    feature_local = residual.shape[1]
    feature_count = feature_local * lax.axis_size("tensor")
    hidden_width = w_down.shape[1]
    expert_count = lax.axis_size("expert")
    capacity = 5 * token_count * topk_count // (4 * expert_count)
    attention = _reduce_scatter(attn_partial[0], 1)
    stream = residual.astype(jnp.float32) + attention
    squares = _psum(jnp.sum(stream * stream, axis=1))
    inverse = lax.rsqrt(squares / feature_count + 1e-06)[:, None]
    normed = stream * inverse * norm_gain[None, :]
    rows = normed.astype(jnp.bfloat16)
    flat_ids = expert_ids.reshape(-1)
    one_hot = (flat_ids[:, None] == jnp.arange(expert_count, dtype=jnp.int32)[None, :]).astype(
        jnp.int32
    )
    earlier = jnp.cumsum(one_hot, axis=0) - one_hot
    slot_index = jnp.sum(earlier * one_hot, axis=1)
    positions = (flat_ids * capacity + slot_index).reshape(token_count, topk_count)
    places = jnp.arange(expert_count * capacity, dtype=jnp.int32)
    matches = positions[None, :, :] == places[:, None, None]
    dispatch = jnp.any(matches, axis=2)
    sent_rows = jnp.dot(dispatch.astype(jnp.bfloat16), rows, preferred_element_type=jnp.float32)
    sent_rows = sent_rows.astype(jnp.bfloat16).reshape(expert_count, capacity, feature_local)
    weights_table = jnp.sum(jnp.where(matches, route_weight[None, :, :], 0.0), axis=2).T
    in_rows = _exchange_rows(sent_rows)
    source_count = in_rows.shape[0]
    item_count = in_rows.shape[1]
    row_total = source_count * item_count
    flat_rows = in_rows.reshape(row_total, feature_local)
    t = lax.axis_index("tensor")
    core = t % 2
    high = t // 2
    block = row_total // 4
    away_rows = _slab(flat_rows, 2 * (1 - core) * block, 2 * block, 0)
    home_rows = _slab(flat_rows, 2 * core * block, 2 * block, 0)
    sent = jnp.dot(away_rows, w_in[0], preferred_element_type=jnp.float32).astype(jnp.bfloat16)
    home_rows, sent = lax.optimization_barrier((home_rows, sent))
    received = _exchange(sent, 1)
    kept = jnp.dot(home_rows, w_in[0], preferred_element_type=jnp.float32).astype(jnp.bfloat16)
    away = _slab(kept, (1 - high) * block, block, 0).astype(jnp.float32)
    away = away + _slab(received, (1 - high) * block, block, 0).astype(jnp.float32)
    far = _exchange(away.astype(jnp.bfloat16), 2)
    home = _slab(kept, high * block, block, 0).astype(jnp.float32)
    home = lax.optimization_barrier(home + _slab(received, high * block, block, 0).astype(jnp.float32))
    total = home + far.astype(jnp.float32)
    hidden = (jax.nn.silu(total[:, :hidden_width]) * total[:, hidden_width:]).astype(jnp.bfloat16)
    hidden = _all_gather_rows(hidden)
    produced = jnp.dot(hidden, w_down[0], preferred_element_type=jnp.float32).astype(jnp.bfloat16)
    results = produced.reshape(source_count, item_count, feature_local)
    returned = _exchange_rows(results)
    routed = jnp.dot(
        weights_table,
        returned.reshape(expert_count * capacity, feature_local).astype(jnp.float32),
        precision=lax.Precision.HIGH,
    )
    return (stream + routed).astype(jnp.bfloat16)


def solution(mesh):
    in_specs = (
        P("tensor", "expert", None),
        P("expert", "tensor"),
        P("tensor"),
        P("expert", None),
        P("expert", None),
        P("expert", "tensor", None),
        P("expert", None, "tensor"),
    )
    out_specs = P("expert", "tensor")
    return jax.shard_map(_body, mesh=mesh, in_specs=in_specs, out_specs=out_specs, check_vma=False)
```

```python
import jax
import jax.numpy as jnp
from jax import lax
from jax.sharding import PartitionSpec as P


def _exchange(value, flip):
    size = lax.axis_size("tensor")
    return lax.ppermute(value, "tensor", [(j, j ^ flip) for j in range(size)])


def _slab(value, start, size, axis):
    return lax.dynamic_slice_in_dim(value, start, size, axis=axis)


def _reduce_scatter(value, axis):
    t = lax.axis_index("tensor")
    core = t % 2
    high = t // 2
    n = value.shape[axis] // 4
    sent = jnp.concatenate(
        [_slab(value, (1 - core) * n, n, axis), _slab(value, (3 - core) * n, n, axis)], axis
    ).astype(jnp.bfloat16)
    received = _exchange(sent, 1)
    away = _slab(value, (3 - 2 * high + core - 1) * n, n, axis).astype(jnp.float32)
    away = away + _slab(received, (1 - high) * n, n, axis).astype(jnp.float32)
    home = _slab(value, (2 * high + core) * n, n, axis).astype(jnp.float32)
    home = home + _slab(received, high * n, n, axis).astype(jnp.float32)
    return home + _exchange(away.astype(jnp.bfloat16), 2).astype(jnp.float32)


def _exchange_rows(value):
    experts, slots, features = value.shape
    lanes = 128
    packed = value.reshape(experts, slots * features // lanes, lanes)
    moved = lax.all_to_all(packed, "expert", split_axis=0, concat_axis=0, tiled=True)
    return moved.reshape(experts, slots, features)


def _psum(value):
    value = value + _exchange(value, 1)
    return value + _exchange(value, 2)


def _body(attn_partial, residual, norm_gain, expert_ids, route_weight, w_in, w_down):
    token_count = expert_ids.shape[0]
    topk_count = expert_ids.shape[1]
    feature_local = residual.shape[1]
    feature_count = feature_local * lax.axis_size("tensor")
    hidden_width = w_down.shape[1]
    expert_count = lax.axis_size("expert")
    capacity = 5 * token_count * topk_count // (4 * expert_count)
    attention = _reduce_scatter(attn_partial[0], 1)
    stream = residual.astype(jnp.float32) + attention
    squares = _psum(jnp.sum(stream * stream, axis=1))
    inverse = lax.rsqrt(squares / feature_count + 1e-06)[:, None]
    normed = stream * inverse * norm_gain[None, :]
    rows = normed.astype(jnp.bfloat16)
    flat_ids = expert_ids.reshape(-1)
    one_hot = (flat_ids[:, None] == jnp.arange(expert_count, dtype=jnp.int32)[None, :]).astype(
        jnp.int32
    )
    earlier = jnp.cumsum(one_hot, axis=0) - one_hot
    slot_index = jnp.sum(earlier * one_hot, axis=1)
    positions = (flat_ids * capacity + slot_index).reshape(token_count, topk_count)
    places = jnp.arange(expert_count * capacity, dtype=jnp.int32)
    matches = positions[None, :, :] == places[:, None, None]
    dispatch = jnp.any(matches, axis=2)
    sent_rows = jnp.dot(dispatch.astype(jnp.bfloat16), rows, preferred_element_type=jnp.float32)
    sent_rows = sent_rows.astype(jnp.bfloat16).reshape(expert_count, capacity, feature_local)
    weights_table = jnp.sum(jnp.where(matches, route_weight[None, :, :], 0.0), axis=2).T
    in_rows = _exchange_rows(sent_rows)
    source_count = in_rows.shape[0]
    item_count = in_rows.shape[1]
    row_total = source_count * item_count
    flat_rows = in_rows.reshape(row_total, feature_local)
    t = lax.axis_index("tensor")
    core = t % 2
    high = t // 2
    block = row_total // 4
    away_rows = _slab(flat_rows, 2 * (1 - core) * block, 2 * block, 0)
    home_rows = _slab(flat_rows, 2 * core * block, 2 * block, 0)
    sent = jnp.dot(away_rows, w_in[0], preferred_element_type=jnp.float32).astype(jnp.bfloat16)
    home_rows, sent = lax.optimization_barrier((home_rows, sent))
    received = _exchange(sent, 1)
    kept = jnp.dot(home_rows, w_in[0], preferred_element_type=jnp.float32).astype(jnp.bfloat16)
    away = _slab(kept, (1 - high) * block, block, 0).astype(jnp.float32)
    away = away + _slab(received, (1 - high) * block, block, 0).astype(jnp.float32)
    far = _exchange(away.astype(jnp.bfloat16), 2)
    home = _slab(kept, high * block, block, 0).astype(jnp.float32)
    home = lax.optimization_barrier(home + _slab(received, high * block, block, 0).astype(jnp.float32))
    total = home + far.astype(jnp.float32)
    hidden = (jax.nn.silu(total[:, :hidden_width]) * total[:, hidden_width:]).astype(jnp.bfloat16)
    n = hidden.shape[0]
    pair = jnp.zeros((2 * n,) + hidden.shape[1:], hidden.dtype)
    pair = lax.dynamic_update_slice_in_dim(pair, hidden, high * n, 0)
    pair = lax.dynamic_update_slice_in_dim(pair, _exchange(hidden, 2), (1 - high) * n, 0)
    pair = lax.optimization_barrier(pair)
    other = _exchange(pair, 1)
    near = jnp.dot(pair, w_down[0], preferred_element_type=jnp.float32).astype(jnp.bfloat16)
    far_out = jnp.dot(other, w_down[0], preferred_element_type=jnp.float32).astype(jnp.bfloat16)
    produced = jnp.zeros((4 * n, near.shape[1]), near.dtype)
    produced = lax.dynamic_update_slice_in_dim(produced, near, 2 * core * n, 0)
    produced = lax.dynamic_update_slice_in_dim(produced, far_out, 2 * (1 - core) * n, 0)
    results = produced.reshape(source_count, item_count, feature_local)
    returned = _exchange_rows(results)
    routed = jnp.dot(
        weights_table,
        returned.reshape(expert_count * capacity, feature_local).astype(jnp.float32),
        precision=lax.Precision.HIGHEST,
    )
    return (stream + routed).astype(jnp.bfloat16)


def solution(mesh):
    in_specs = (
        P("tensor", "expert", None),
        P("expert", "tensor"),
        P("tensor"),
        P("expert", None),
        P("expert", None),
        P("expert", "tensor", None),
        P("expert", None, "tensor"),
    )
    out_specs = P("expert", "tensor")
    return jax.shard_map(_body, mesh=mesh, in_specs=in_specs, out_specs=out_specs, check_vma=False)
```

```python
import jax
import jax.numpy as jnp
from jax import lax
from jax.sharding import PartitionSpec as P


def _exchange(value, flip):
    size = lax.axis_size("tensor")
    return lax.ppermute(value, "tensor", [(j, j ^ flip) for j in range(size)])


def _slab(value, start, size, axis):
    return lax.dynamic_slice_in_dim(value, start, size, axis=axis)


def _reduce_scatter(value, axis):
    t = lax.axis_index("tensor")
    core = t % 2
    high = t // 2
    n = value.shape[axis] // 4
    sent = jnp.concatenate(
        [_slab(value, (1 - core) * n, n, axis), _slab(value, (3 - core) * n, n, axis)], axis
    ).astype(jnp.bfloat16)
    received = _exchange(sent, 1)
    away = _slab(value, (3 - 2 * high + core - 1) * n, n, axis).astype(jnp.float32)
    away = away + _slab(received, (1 - high) * n, n, axis).astype(jnp.float32)
    home = _slab(value, (2 * high + core) * n, n, axis).astype(jnp.float32)
    home = home + _slab(received, high * n, n, axis).astype(jnp.float32)
    return home + _exchange(away.astype(jnp.bfloat16), 2).astype(jnp.float32)


def _exchange_rows(value):
    experts, slots, features = value.shape
    lanes = 128
    packed = value.reshape(experts, slots * features // lanes, lanes)
    moved = lax.all_to_all(packed, "expert", split_axis=0, concat_axis=0, tiled=True)
    return moved.reshape(experts, slots, features)


def _psum(value):
    value = value + _exchange(value, 1)
    return value + _exchange(value, 2)


def _body(attn_partial, residual, norm_gain, expert_ids, route_weight, w_in, w_down):
    token_count = expert_ids.shape[0]
    topk_count = expert_ids.shape[1]
    feature_local = residual.shape[1]
    feature_count = feature_local * lax.axis_size("tensor")
    hidden_width = w_down.shape[1]
    expert_count = lax.axis_size("expert")
    capacity = 5 * token_count * topk_count // (4 * expert_count)
    attention = _reduce_scatter(attn_partial[0], 1)
    stream = residual.astype(jnp.float32) + attention
    squares = _psum(jnp.sum(stream * stream, axis=1))
    inverse = lax.rsqrt(squares / feature_count + 1e-06)[:, None]
    normed = stream * inverse * norm_gain[None, :]
    rows = normed.astype(jnp.bfloat16)
    flat_ids = expert_ids.reshape(-1)
    one_hot = (flat_ids[:, None] == jnp.arange(expert_count, dtype=jnp.int32)[None, :]).astype(
        jnp.int32
    )
    earlier = jnp.cumsum(one_hot, axis=0) - one_hot
    slot_index = jnp.sum(earlier * one_hot, axis=1)
    positions = (flat_ids * capacity + slot_index).reshape(token_count, topk_count)
    places = jnp.arange(expert_count * capacity, dtype=jnp.int32)
    matches = positions[None, :, :] == places[:, None, None]
    dispatch = jnp.any(matches, axis=2)
    sent_rows = jnp.dot(dispatch.astype(jnp.bfloat16), rows, preferred_element_type=jnp.float32)
    sent_rows = sent_rows.astype(jnp.bfloat16).reshape(expert_count, capacity, feature_local)
    weights_table = jnp.sum(jnp.where(matches, route_weight[None, :, :], 0.0), axis=2).T
    in_rows = _exchange_rows(sent_rows)
    source_count = in_rows.shape[0]
    item_count = in_rows.shape[1]
    row_total = source_count * item_count
    flat_rows = in_rows.reshape(row_total, feature_local)
    t = lax.axis_index("tensor")
    core = t % 2
    high = t // 2
    block = row_total // 4
    away_rows = _slab(flat_rows, 2 * (1 - core) * block, 2 * block, 0)
    home_rows = _slab(flat_rows, 2 * core * block, 2 * block, 0)
    sent = jnp.dot(away_rows, w_in[0], preferred_element_type=jnp.float32).astype(jnp.bfloat16)
    home_rows, sent = lax.optimization_barrier((home_rows, sent))
    received = _exchange(sent, 1)
    kept = jnp.dot(home_rows, w_in[0], preferred_element_type=jnp.float32).astype(jnp.bfloat16)
    away = _slab(kept, (1 - high) * block, block, 0).astype(jnp.float32)
    away = away + _slab(received, (1 - high) * block, block, 0).astype(jnp.float32)
    far = _exchange(away.astype(jnp.bfloat16), 2)
    home = _slab(kept, high * block, block, 0).astype(jnp.float32)
    home = lax.optimization_barrier(home + _slab(received, high * block, block, 0).astype(jnp.float32))
    total = home + far.astype(jnp.float32)
    hidden = (jax.nn.silu(total[:, :hidden_width]) * total[:, hidden_width:]).astype(jnp.bfloat16)
    n = hidden.shape[0]
    pair = jnp.zeros((2 * n,) + hidden.shape[1:], hidden.dtype)
    pair = lax.dynamic_update_slice_in_dim(pair, hidden, high * n, 0)
    beside = _exchange(hidden, 2)
    own_out = jnp.dot(hidden, w_down[0], preferred_element_type=jnp.float32).astype(jnp.bfloat16)
    pair = lax.dynamic_update_slice_in_dim(pair, beside, (1 - high) * n, 0)
    pair = lax.optimization_barrier(pair)
    other = _exchange(pair, 1)
    beside_out = jnp.dot(beside, w_down[0], preferred_element_type=jnp.float32).astype(jnp.bfloat16)
    far_out = jnp.dot(other, w_down[0], preferred_element_type=jnp.float32).astype(jnp.bfloat16)
    produced = jnp.zeros((4 * n, own_out.shape[1]), own_out.dtype)
    produced = lax.dynamic_update_slice_in_dim(produced, own_out, (2 * core + high) * n, 0)
    produced = lax.dynamic_update_slice_in_dim(produced, beside_out, (2 * core + 1 - high) * n, 0)
    produced = lax.dynamic_update_slice_in_dim(produced, far_out, 2 * (1 - core) * n, 0)
    results = produced.reshape(source_count, item_count, feature_local)
    returned = _exchange_rows(results)
    routed = jnp.dot(
        weights_table,
        returned.reshape(expert_count * capacity, feature_local).astype(jnp.float32),
        precision=lax.Precision.HIGHEST,
    )
    return (stream + routed).astype(jnp.bfloat16)


def solution(mesh):
    in_specs = (
        P("tensor", "expert", None),
        P("expert", "tensor"),
        P("tensor"),
        P("expert", None),
        P("expert", None),
        P("expert", "tensor", None),
        P("expert", None, "tensor"),
    )
    out_specs = P("expert", "tensor")
    return jax.shard_map(_body, mesh=mesh, in_specs=in_specs, out_specs=out_specs, check_vma=False)
```
